512 devices in a mesh: gx: 8 (over x, core), gy: 4 (over y), gz: 16 (over z).
Axes of the slice: x: 4, y: 4, z: 16, core: 2. Of those that a mesh axis runs over, the one named last changes fastest.
Arguments:
- multipoles: bfloat16 [289, 262144], P(None, ('gx', 'gy', 'gz')), may hold values from -6 to 6
- up_shift: bfloat16 [8, 289, 289], replicated, may hold values from -0.125 to 0.125
- down_shift: bfloat16 [8, 289, 289], replicated, may hold values from -0.375 to 0.375
- far_shift: bfloat16 [8, 289, 289], replicated, may hold values from -0.09375 to 0.09375
- send_list: int32 [8, 64, 64, 16], P('gx', ('gy', 'gz')), may hold values from 0 to 511
- leaf_src: int32 [16, 262144], P(None, ('gx', 'gy', 'gz')), may hold values from 0 to 1535
- leaf_kind: int32 [16, 262144], P(None, ('gx', 'gy', 'gz')), may hold values from 0 to 7
- coarse_src: int32 [8, 64], replicated, may hold values from 0 to 63
- coarse_kind: int32 [8, 64], replicated, may hold values from 0 to 7
Outputs:
- leaf_local: bfloat16 [289, 262144], P(None, ('gx', 'gy', 'gz'))
The draws below stay inside these ranges and needn't reach their ends.
All inputs are finite; a program needn't handle non-finite values.
Results may differ from the reference program's by a relative error of at most 0.014.
Values may be sent and summed in bfloat16 or wider, within the bound.
No kernel may reach another device: no remote copies, remote signals or barrier semaphores. Data moves between devices by JAX's collectives and lax.ppermute only.
A program may use at most 128 MiB of HBM per device.

```python
import math
import jax
import jax.numpy as jnp
import numpy as np
from jax import lax

P2 = 289
LOCAL_LEVELS = 3
KINDS = 8
LIST = 16
CL = 8
SLOT = 16
LEAF_DEV = 512
PEERS = 64
LEAVES = 262144
NBUF = 1536
COARSE = 64
N_GX = 8
N_GY = 4
N_GZ = 16


def with_ends(values, stream_key, least, largest):
    longest = values.shape.index(max(values.shape))
    spots = []
    for shift in (0, 1):
        where = [jax.random.randint(jax.random.fold_in(stream_key, axis), (), 0, length) for axis, length in enumerate(values.shape)]
        where[longest] = (where[longest] + shift) % values.shape[longest]
        spots.append(tuple(where))
    return values.at[spots[0]].set(least).at[spots[1]].set(largest)


def level_of(own_key, shape, cuts, smallest, top_value):
    def one(dim, blocks):
        draws = jax.random.uniform(jax.random.fold_in(jax.random.fold_in(own_key, 6), dim), (blocks,), jnp.float32, smallest / len(cuts), top_value / len(cuts))
        return jnp.repeat(jnp.exp(draws), shape[dim] // blocks).reshape((-1,) + (1,) * (len(shape) - dim - 1))

    loudness = one(*cuts[0])
    for cut in cuts[1:]:
        loudness = loudness * one(*cut)
    return loudness


def rank_bounds(number_of, skew):
    weights = [(1 << 20) // math.isqrt(rank ** skew) + 1 for rank in range(1, number_of + 1)]
    scale = 1 + sum(weights) // (1 << 30)
    return np.cumsum(np.array([max(1, weight // scale) for weight in weights]))


def skewed_ids(stream_key, shape, count, skew):
    listing = rank_bounds(count, skew)
    pick = jax.random.randint(jax.random.fold_in(stream_key, 1), shape, 0, int(listing[count - 1]))
    standing = jnp.searchsorted(jnp.asarray(listing, jnp.int32), pick, side="right")
    return jax.random.permutation(jax.random.fold_in(stream_key, 2), count)[standing].astype(jnp.int32)


def scatter_about(key, extent, scale, bound, cuts=(), held_as=jnp.bfloat16):
    values = scale * jax.random.normal(key, extent, jnp.float32)
    if cuts:
        values = values * level_of(key, extent, cuts, -0.22, 0.18)
    return jnp.clip(values, -bound, bound).astype(held_as)


def setup_inputs(seed: int = 0) -> dict:
    arg_keys = jax.random.split(jax.random.key(seed), 10)
    multipoles = scatter_about(arg_keys[0], (P2, LEAVES), 1.0, 6.0, ((1, 512),))
    up_shift = scatter_about(arg_keys[1], (8, P2, P2), (8 * P2) ** -0.5, 0.125)
    down_shift = scatter_about(arg_keys[2], (8, P2, P2), P2 ** -0.5, 0.375)
    far_shift = scatter_about(arg_keys[3], (KINDS, P2, P2), (LIST * P2) ** -0.5, 0.09375)
    send_list = with_ends(skewed_ids(arg_keys[4], (N_GX, PEERS, PEERS, SLOT), LEAF_DEV, 2), jax.random.fold_in(arg_keys[4], 3), 0, LEAF_DEV - 1).astype(jnp.int32)
    leaf_src = with_ends(jax.random.randint(arg_keys[5], (LIST, LEAVES), 0, NBUF), jax.random.fold_in(arg_keys[5], 1), 0, NBUF - 1).astype(jnp.int32)
    leaf_kind = with_ends(jax.random.randint(arg_keys[6], (LIST, LEAVES), 0, KINDS), jax.random.fold_in(arg_keys[6], 1), 0, KINDS - 1).astype(jnp.int32)
    coarse_src = with_ends(jax.random.randint(arg_keys[7], (CL, COARSE), 0, COARSE), jax.random.fold_in(arg_keys[7], 1), 0, COARSE - 1).astype(jnp.int32)
    coarse_kind = with_ends(jax.random.randint(arg_keys[8], (CL, COARSE), 0, KINDS), jax.random.fold_in(arg_keys[8], 1), 0, KINDS - 1).astype(jnp.int32)
    return {"multipoles": multipoles, "up_shift": up_shift, "down_shift": down_shift, "far_shift": far_shift, "send_list": send_list, "leaf_src": leaf_src, "leaf_kind": leaf_kind, "coarse_src": coarse_src, "coarse_kind": coarse_kind}


def lift_level(children, up_shift):
    count = children.shape[1] // 8
    child_stack = children.reshape(P2, count, 8).transpose(2, 0, 1).reshape(8 * P2, count)
    shift_table = up_shift.transpose(1, 0, 2).reshape(P2, 8 * P2)
    return jnp.dot(shift_table, child_stack, preferred_element_type=jnp.float32)


def lower_level(parent, down_shift):
    count = parent.shape[1]
    spread = jnp.dot(down_shift.reshape(8 * P2, P2), parent, preferred_element_type=jnp.float32)
    return spread.reshape(8, P2, count).transpose(1, 2, 0).reshape(P2, 8 * count)


def sum_by_kind(picked, kind_ids, far_shift):
    far_total = jnp.zeros((picked.shape[1], picked.shape[2]), jnp.float32)
    for kind in range(KINDS):
        kind_mask = (kind_ids == kind)[:, None, :]
        grouped = jnp.sum(jnp.where(kind_mask, picked.astype(jnp.float32), jnp.float32(0.0)), axis=0)
        far_total = far_total + jnp.dot(far_shift[kind].astype(jnp.float32), grouped, precision=lax.Precision.HIGHEST)
    return far_total


def reference(multipoles, up_shift, down_shift, far_shift, send_list, leaf_src, leaf_kind, coarse_src, coarse_kind):
    devices = N_GX * N_GY * N_GZ
    upward = multipoles
    for level in range(LOCAL_LEVELS):
        upward = lift_level(upward, up_shift).astype(jnp.bfloat16)
    coarse_multi = lift_level(upward, up_shift).astype(jnp.bfloat16)
    coarse_picked = coarse_multi[:, coarse_src].transpose(1, 0, 2)
    coarse_local = sum_by_kind(coarse_picked, coarse_kind, far_shift).astype(jnp.bfloat16)
    downward = lower_level(coarse_local, down_shift).astype(jnp.bfloat16)
    for level in range(LOCAL_LEVELS - 1):
        downward = lower_level(downward, down_shift).astype(jnp.bfloat16)
    chain_part = lower_level(downward, down_shift)

    def one_device(device):
        row_group = device // PEERS
        column = device % PEERS
        own_leaves = device * LEAF_DEV + jnp.arange(LEAF_DEV, dtype=jnp.int32)
        sent_rows = send_list[row_group, :, column, :]
        ghost_rows = (row_group * PEERS + jnp.arange(PEERS, dtype=jnp.int32))[:, None] * LEAF_DEV + sent_rows
        source_buffer = jnp.concatenate([own_leaves, ghost_rows.reshape(PEERS * SLOT).astype(jnp.int32)]).astype(jnp.int32)
        local_src = lax.dynamic_slice_in_dim(leaf_src, (device * LEAF_DEV).astype(jnp.int32), LEAF_DEV, 1)
        kind_ids = lax.dynamic_slice_in_dim(leaf_kind, (device * LEAF_DEV).astype(jnp.int32), LEAF_DEV, 1)
        global_src = source_buffer[local_src]
        picked = multipoles[:, global_src].transpose(1, 0, 2)
        return sum_by_kind(picked, kind_ids, far_shift)

    far = lax.map(one_device, jnp.arange(devices, dtype=jnp.int32))
    far = far.transpose(1, 0, 2).reshape(P2, devices * LEAF_DEV)
    return (chain_part + far).astype(jnp.bfloat16)
```

```python
import jax
import jax.numpy as jnp
from jax import lax
from jax.sharding import PartitionSpec as P

LOCAL_LEVELS = 3


def lift_level(children, up_shift):
    coefs = children.shape[0]
    count = children.shape[1] // 8
    child_stack = children.reshape(coefs, count, 8).transpose(2, 0, 1).reshape(8 * coefs, count)
    shift_table = up_shift.transpose(1, 0, 2).reshape(coefs, 8 * coefs)
    return jnp.dot(shift_table, child_stack, preferred_element_type=jnp.float32)


def lower_level(parent, down_shift):
    coefs = parent.shape[0]
    count = parent.shape[1]
    spread = jnp.dot(
        down_shift.reshape(8 * coefs, coefs), parent, preferred_element_type=jnp.float32
    )
    return spread.reshape(8, coefs, count).transpose(1, 2, 0).reshape(coefs, 8 * count)


def gather_columns(column_block, axes):
    group = lax.axis_size(axes)
    width = column_block.shape[1]
    spread = jnp.broadcast_to(column_block[:, None, :], (column_block.shape[0], group, width))
    spread = spread.reshape(column_block.shape[0], group * width)
    return lax.all_to_all(spread, axes, split_axis=1, concat_axis=1, tiled=True)


def on_device(
    multipoles,
    up_shift,
    down_shift,
    far_shift,
    send_list,
    leaf_src,
    leaf_kind,
    coarse_src,
    coarse_kind,
):
    coefs = multipoles.shape[0]
    kind_count = far_shift.shape[0]
    flat_index = lax.axis_index(("gx", "gy", "gz"))
    coarse_box = flat_index // 8
    octant = flat_index % 8
    peer_count = lax.axis_size(("gy", "gz"))
    slot_count = send_list.shape[3]
    send_order = send_list.reshape(peer_count * slot_count)
    outgoing = jnp.take(multipoles, send_order, axis=1)
    arrived = lax.all_to_all(outgoing, ("gy", "gz"), split_axis=1, concat_axis=1, tiled=True)
    upward = multipoles
    for level in range(LOCAL_LEVELS):
        upward = lift_level(upward, up_shift).astype(jnp.bfloat16)
    row_boxes = gather_columns(upward, "gz")
    row_multi = lift_level(row_boxes, up_shift).astype(jnp.bfloat16)
    coarse_multi = gather_columns(row_multi, ("gx", "gy"))
    coarse_cols = coarse_src[:, coarse_box]
    coarse_kinds = coarse_kind[:, coarse_box]
    list_len = coarse_cols.shape[0]
    coarse_picked = jnp.take(coarse_multi, coarse_cols, axis=1)
    stacked = (
        jnp.take(far_shift, coarse_kinds, axis=0)
        .transpose(1, 0, 2)
        .reshape(coefs, list_len * coefs)
    )
    column_vec = coarse_picked.transpose(1, 0).reshape(list_len * coefs, 1)
    coarse_local = jnp.dot(stacked, column_vec, preferred_element_type=jnp.float32).astype(
        jnp.bfloat16
    )
    downward = jnp.dot(down_shift[octant], coarse_local, preferred_element_type=jnp.float32).astype(
        jnp.bfloat16
    )
    for level in range(LOCAL_LEVELS - 1):
        downward = lower_level(downward, down_shift).astype(jnp.bfloat16)
    chain_part = lower_level(downward, down_shift)
    buffer = jnp.concatenate([multipoles, arrived], axis=1)
    leaf_count = leaf_src.shape[1]
    picked = jnp.take(buffer, leaf_src, axis=1)
    kind_range = jnp.arange(kind_count, dtype=jnp.int32)
    kind_hot = (leaf_kind[None, :, :] == kind_range[:, None, None]).astype(jnp.bfloat16)
    grouped = jnp.einsum("plt,klt->kpt", picked, kind_hot, preferred_element_type=jnp.float32)
    grouped = grouped.reshape(kind_count * coefs, leaf_count)
    upper_part = grouped.astype(jnp.bfloat16)
    lower_part = (grouped - upper_part.astype(jnp.float32)).astype(jnp.bfloat16)
    shift_table = far_shift.transpose(1, 0, 2).reshape(coefs, kind_count * coefs)
    far_total = jnp.dot(shift_table, upper_part, preferred_element_type=jnp.float32)
    far_total = far_total + jnp.dot(shift_table, lower_part, preferred_element_type=jnp.float32)
    return (chain_part + far_total).astype(jnp.bfloat16)


def solution(mesh):
    in_specs = (
        P(None, ("gx", "gy", "gz")),
        P(),
        P(),
        P(),
        P("gx", ("gy", "gz"), None, None),
        P(None, ("gx", "gy", "gz")),
        P(None, ("gx", "gy", "gz")),
        P(),
        P(),
    )
    out_specs = P(None, ("gx", "gy", "gz"))
    return jax.shard_map(
        on_device, mesh=mesh, in_specs=in_specs, out_specs=out_specs, check_vma=False
    )
```

```python
import jax
import jax.numpy as jnp
from jax import lax
from jax.experimental import pallas as pl
from jax.experimental.pallas import tpu as pltpu
from jax.sharding import PartitionSpec as P

LOCAL_LEVELS = 3
LANES = 384


def lift_level(children, up_shift):
    coefs = children.shape[0]
    count = children.shape[1] // 8
    child_stack = children.reshape(coefs, count, 8).transpose(2, 0, 1).reshape(8 * coefs, count)
    shift_table = up_shift.transpose(1, 0, 2).reshape(coefs, 8 * coefs)
    return jnp.dot(shift_table, child_stack, preferred_element_type=jnp.float32)


def lower_level(parent, down_shift):
    coefs = parent.shape[0]
    count = parent.shape[1]
    spread = jnp.dot(
        down_shift.reshape(8 * coefs, coefs), parent, preferred_element_type=jnp.float32
    )
    return spread.reshape(8, coefs, count).transpose(1, 2, 0).reshape(coefs, 8 * count)


def far_kernel(idx_ref, buf_ref, fs_ref, out_ref, table_ref):
    kinds = fs_ref.shape[0]
    rows = buf_ref.shape[0]
    for k in range(kinds):
        table_ref[pl.ds(k * rows, rows), :] = jnp.dot(
            buf_ref[...], fs_ref[k], preferred_element_type=jnp.float32
        )
    targets = out_ref.shape[0]
    lists = idx_ref.shape[0] // targets

    def body(t, carry):
        base = t * lists
        acc = table_ref[pl.ds(idx_ref[base], 1), :]
        for l in range(1, lists):
            acc = acc + table_ref[pl.ds(idx_ref[base + l], 1), :]
        out_ref[pl.ds(t, 1), :] = acc
        return carry

    lax.fori_loop(0, targets, body, 0)


def far_field(buffer, far_shift, leaf_src, leaf_kind):
    coefs, rows = buffer.shape
    kinds = far_shift.shape[0]
    lists, targets = leaf_src.shape
    pad = LANES - coefs
    buf_t = jnp.pad(buffer.T, ((0, 0), (0, pad)))
    fs_t = jnp.pad(far_shift.transpose(0, 2, 1), ((0, 0), (0, pad), (0, pad)))
    idx = (leaf_kind * rows + leaf_src).T.reshape(lists * targets)
    out = pl.pallas_call(
        far_kernel,
        out_shape=jax.ShapeDtypeStruct((targets, LANES), jnp.float32),
        in_specs=[
            pl.BlockSpec(memory_space=pltpu.SMEM),
            pl.BlockSpec(memory_space=pltpu.VMEM),
            pl.BlockSpec(memory_space=pltpu.VMEM),
        ],
        out_specs=pl.BlockSpec(memory_space=pltpu.VMEM),
        scratch_shapes=[pltpu.VMEM((kinds * rows, LANES), jnp.float32)],
    )(idx, buf_t, fs_t)
    return out[:, :coefs].T


def gather_columns(column_block, axes):
    group = lax.axis_size(axes)
    width = column_block.shape[1]
    spread = jnp.broadcast_to(column_block[:, None, :], (column_block.shape[0], group, width))
    spread = spread.reshape(column_block.shape[0], group * width)
    return lax.all_to_all(spread, axes, split_axis=1, concat_axis=1, tiled=True)


def on_device(
    multipoles,
    up_shift,
    down_shift,
    far_shift,
    send_list,
    leaf_src,
    leaf_kind,
    coarse_src,
    coarse_kind,
):
    coefs = multipoles.shape[0]
    flat_index = lax.axis_index(("gx", "gy", "gz"))
    coarse_box = flat_index // 8
    octant = flat_index % 8
    peer_count = lax.axis_size(("gy", "gz"))
    slot_count = send_list.shape[3]
    send_order = send_list.reshape(peer_count * slot_count)
    outgoing = jnp.take(multipoles, send_order, axis=1)
    arrived = lax.all_to_all(outgoing, ("gy", "gz"), split_axis=1, concat_axis=1, tiled=True)
    upward = multipoles
    for level in range(LOCAL_LEVELS):
        upward = lift_level(upward, up_shift).astype(jnp.bfloat16)
    row_boxes = gather_columns(upward, "gz")
    row_multi = lift_level(row_boxes, up_shift).astype(jnp.bfloat16)
    coarse_multi = gather_columns(row_multi, ("gx", "gy"))
    coarse_cols = coarse_src[:, coarse_box]
    coarse_kinds = coarse_kind[:, coarse_box]
    list_len = coarse_cols.shape[0]
    coarse_picked = jnp.take(coarse_multi, coarse_cols, axis=1)
    stacked = (
        jnp.take(far_shift, coarse_kinds, axis=0)
        .transpose(1, 0, 2)
        .reshape(coefs, list_len * coefs)
    )
    column_vec = coarse_picked.transpose(1, 0).reshape(list_len * coefs, 1)
    coarse_local = jnp.dot(stacked, column_vec, preferred_element_type=jnp.float32).astype(
        jnp.bfloat16
    )
    downward = jnp.dot(down_shift[octant], coarse_local, preferred_element_type=jnp.float32).astype(
        jnp.bfloat16
    )
    for level in range(LOCAL_LEVELS - 1):
        downward = lower_level(downward, down_shift).astype(jnp.bfloat16)
    chain_part = lower_level(downward, down_shift)
    buffer = jnp.concatenate([multipoles, arrived], axis=1)
    far_total = far_field(buffer, far_shift, leaf_src, leaf_kind)
    return (chain_part + far_total).astype(jnp.bfloat16)


def solution(mesh):
    in_specs = (
        P(None, ("gx", "gy", "gz")),
        P(),
        P(),
        P(),
        P("gx", ("gy", "gz"), None, None),
        P(None, ("gx", "gy", "gz")),
        P(None, ("gx", "gy", "gz")),
        P(),
        P(),
    )
    out_specs = P(None, ("gx", "gy", "gz"))
    return jax.shard_map(
        on_device, mesh=mesh, in_specs=in_specs, out_specs=out_specs, check_vma=False
    )
```

```python
import jax
import jax.numpy as jnp
from jax import lax
from jax.experimental import pallas as pl
from jax.experimental.pallas import tpu as pltpu
from jax.sharding import PartitionSpec as P

LOCAL_LEVELS = 3
LANES = 384


def lift_level(children, up_shift):
    coefs = children.shape[0]
    count = children.shape[1] // 8
    child_stack = children.reshape(coefs, count, 8).transpose(2, 0, 1).reshape(8 * coefs, count)
    shift_table = up_shift.transpose(1, 0, 2).reshape(coefs, 8 * coefs)
    return jnp.dot(shift_table, child_stack, preferred_element_type=jnp.float32)


def lower_level(parent, down_shift):
    coefs = parent.shape[0]
    count = parent.shape[1]
    spread = jnp.dot(
        down_shift.reshape(8 * coefs, coefs), parent, preferred_element_type=jnp.float32
    )
    return spread.reshape(8, coefs, count).transpose(1, 2, 0).reshape(coefs, 8 * count)


def far_kernel(idx_ref, buf_ref, fs_ref, out_ref, table_ref):
    kinds = fs_ref.shape[0]
    rows = buf_ref.shape[0]
    for k in range(kinds):
        table_ref[pl.ds(k * rows, rows), :] = jnp.dot(
            buf_ref[...], fs_ref[k], preferred_element_type=jnp.float32
        )
    targets = out_ref.shape[0]
    lists = idx_ref.shape[0] // targets

    def body(t, carry):
        base = t * lists
        acc = table_ref[pl.ds(idx_ref[base], 1), :]
        for l in range(1, lists):
            acc = acc + table_ref[pl.ds(idx_ref[base + l], 1), :]
        out_ref[pl.ds(t, 1), :] = acc
        return carry

    lax.fori_loop(0, targets, body, 0)


def far_field(buffer, far_shift, leaf_src, leaf_kind):
    coefs, rows = buffer.shape
    kinds = far_shift.shape[0]
    lists, targets = leaf_src.shape
    pad = LANES - coefs
    buf_t = jnp.pad(buffer.T, ((0, 0), (0, pad)))
    fs_t = jnp.pad(far_shift.transpose(0, 2, 1), ((0, 0), (0, pad), (0, pad)))
    idx = (leaf_kind * rows + leaf_src).T.reshape(lists * targets)
    out = pl.pallas_call(
        far_kernel,
        out_shape=jax.ShapeDtypeStruct((targets, LANES), jnp.float32),
        in_specs=[
            pl.BlockSpec(memory_space=pltpu.SMEM),
            pl.BlockSpec(memory_space=pltpu.VMEM),
            pl.BlockSpec(memory_space=pltpu.VMEM),
        ],
        out_specs=pl.BlockSpec(memory_space=pltpu.VMEM),
        scratch_shapes=[pltpu.VMEM((kinds * rows, LANES), jnp.float32)],
    )(idx, buf_t, fs_t)
    return out[:, :coefs].T


def gather_columns(column_block, axes):
    return lax.all_gather(column_block, axes, axis=1, tiled=True)


def on_device(
    multipoles,
    up_shift,
    down_shift,
    far_shift,
    send_list,
    leaf_src,
    leaf_kind,
    coarse_src,
    coarse_kind,
):
    coefs = multipoles.shape[0]
    flat_index = lax.axis_index(("gx", "gy", "gz"))
    coarse_box = flat_index // 8
    octant = flat_index % 8
    peer_count = lax.axis_size(("gy", "gz"))
    slot_count = send_list.shape[3]
    send_order = send_list.reshape(peer_count * slot_count)
    outgoing = jnp.take(multipoles, send_order, axis=1)
    arrived = lax.all_to_all(outgoing, ("gy", "gz"), split_axis=1, concat_axis=1, tiled=True)
    upward = multipoles
    for level in range(LOCAL_LEVELS):
        upward = lift_level(upward, up_shift).astype(jnp.bfloat16)
    row_boxes = gather_columns(upward, "gz")
    row_multi = lift_level(row_boxes, up_shift).astype(jnp.bfloat16)
    coarse_multi = gather_columns(row_multi, ("gx", "gy"))
    coarse_cols = coarse_src[:, coarse_box]
    coarse_kinds = coarse_kind[:, coarse_box]
    list_len = coarse_cols.shape[0]
    coarse_picked = jnp.take(coarse_multi, coarse_cols, axis=1)
    stacked = (
        jnp.take(far_shift, coarse_kinds, axis=0)
        .transpose(1, 0, 2)
        .reshape(coefs, list_len * coefs)
    )
    column_vec = coarse_picked.transpose(1, 0).reshape(list_len * coefs, 1)
    coarse_local = jnp.dot(stacked, column_vec, preferred_element_type=jnp.float32).astype(
        jnp.bfloat16
    )
    downward = jnp.dot(down_shift[octant], coarse_local, preferred_element_type=jnp.float32).astype(
        jnp.bfloat16
    )
    for level in range(LOCAL_LEVELS - 1):
        downward = lower_level(downward, down_shift).astype(jnp.bfloat16)
    chain_part = lower_level(downward, down_shift)
    buffer = jnp.concatenate([multipoles, arrived], axis=1)
    far_total = far_field(buffer, far_shift, leaf_src, leaf_kind)
    return (chain_part + far_total).astype(jnp.bfloat16)


def solution(mesh):
    in_specs = (
        P(None, ("gx", "gy", "gz")),
        P(),
        P(),
        P(),
        P("gx", ("gy", "gz"), None, None),
        P(None, ("gx", "gy", "gz")),
        P(None, ("gx", "gy", "gz")),
        P(),
        P(),
    )
    out_specs = P(None, ("gx", "gy", "gz"))
    return jax.shard_map(
        on_device, mesh=mesh, in_specs=in_specs, out_specs=out_specs, check_vma=False
    )
```

```python
import jax
import jax.numpy as jnp
from jax import lax
from jax.experimental import pallas as pl
from jax.experimental.pallas import tpu as pltpu
from jax.sharding import PartitionSpec as P

LOCAL_LEVELS = 3
LANES = 384


def lift_level(children, up_shift):
    coefs = children.shape[0]
    count = children.shape[1] // 8
    child_stack = children.reshape(coefs, count, 8).transpose(2, 0, 1).reshape(8 * coefs, count)
    shift_table = up_shift.transpose(1, 0, 2).reshape(coefs, 8 * coefs)
    return jnp.dot(shift_table, child_stack, preferred_element_type=jnp.float32)


def lower_level(parent, down_shift):
    coefs = parent.shape[0]
    count = parent.shape[1]
    spread = jnp.dot(
        down_shift.reshape(8 * coefs, coefs), parent, preferred_element_type=jnp.float32
    )
    return spread.reshape(8, coefs, count).transpose(1, 2, 0).reshape(coefs, 8 * count)


def far_kernel(idx_ref, buf_ref, fs_ref, out_ref, table_ref):
    kinds = fs_ref.shape[0]
    rows = buf_ref.shape[0]
    for k in range(kinds):
        table_ref[pl.ds(k * rows, rows), :] = jnp.dot(
            buf_ref[...], fs_ref[k], preferred_element_type=jnp.float32
        )
    targets = out_ref.shape[0]
    lists = idx_ref.shape[0] // targets

    def body(t, carry):
        base = t * lists
        acc = table_ref[pl.ds(idx_ref[base], 1), :]
        for l in range(1, lists):
            acc = acc + table_ref[pl.ds(idx_ref[base + l], 1), :]
        out_ref[pl.ds(t, 1), :] = acc
        return carry

    lax.fori_loop(0, targets, body, 0)


def far_field(buffer, far_shift, leaf_src, leaf_kind):
    coefs, rows = buffer.shape
    kinds = far_shift.shape[0]
    lists, targets = leaf_src.shape
    pad = LANES - coefs
    buf_t = jnp.pad(buffer.T, ((0, 0), (0, pad)))
    fs_t = jnp.pad(far_shift.transpose(0, 2, 1), ((0, 0), (0, pad), (0, pad)))
    idx = (leaf_kind * rows + leaf_src).T.reshape(lists * targets)
    out = pl.pallas_call(
        far_kernel,
        out_shape=jax.ShapeDtypeStruct((targets, LANES), jnp.float32),
        in_specs=[
            pl.BlockSpec(memory_space=pltpu.SMEM),
            pl.BlockSpec(memory_space=pltpu.VMEM),
            pl.BlockSpec(memory_space=pltpu.VMEM),
        ],
        out_specs=pl.BlockSpec(memory_space=pltpu.VMEM),
        scratch_shapes=[pltpu.VMEM((kinds * rows, LANES), jnp.float32)],
    )(idx, buf_t, fs_t)
    return out[:, :coefs].T


def gather_columns(column_block, axes):
    group = lax.axis_size(axes)
    width = column_block.shape[1]
    spread = jnp.broadcast_to(column_block[:, None, :], (column_block.shape[0], group, width))
    spread = spread.reshape(column_block.shape[0], group * width)
    return lax.all_to_all(spread, axes, split_axis=1, concat_axis=1, tiled=True)


def on_device(
    multipoles,
    up_shift,
    down_shift,
    far_shift,
    send_list,
    leaf_src,
    leaf_kind,
    coarse_src,
    coarse_kind,
):
    coefs = multipoles.shape[0]
    flat_index = lax.axis_index(("gx", "gy", "gz"))
    coarse_box = flat_index // 8
    octant = flat_index % 8
    peer_count = lax.axis_size(("gy", "gz"))
    slot_count = send_list.shape[3]
    send_order = send_list.reshape(peer_count * slot_count)
    upward = multipoles
    for level in range(LOCAL_LEVELS):
        upward = lift_level(upward, up_shift).astype(jnp.bfloat16)
    outgoing = jnp.take(multipoles, send_order, axis=1).reshape(coefs, peer_count, slot_count)
    own_box = jnp.broadcast_to(upward[:, None, :], (coefs, peer_count, 1))
    payload = jnp.concatenate([outgoing, own_box], axis=2).reshape(coefs, peer_count * (slot_count + 1))
    landed = lax.all_to_all(payload, ("gy", "gz"), split_axis=1, concat_axis=1, tiled=True)
    landed = landed.reshape(coefs, peer_count, slot_count + 1)
    arrived = landed[:, :, :slot_count].reshape(coefs, peer_count * slot_count)
    slice_boxes = landed[:, :, slot_count]
    slice_multi = lift_level(slice_boxes, up_shift).astype(jnp.bfloat16)
    coarse_multi = gather_columns(slice_multi, "gx")
    coarse_cols = coarse_src[:, coarse_box]
    coarse_kinds = coarse_kind[:, coarse_box]
    list_len = coarse_cols.shape[0]
    coarse_picked = jnp.take(coarse_multi, coarse_cols, axis=1)
    stacked = (
        jnp.take(far_shift, coarse_kinds, axis=0)
        .transpose(1, 0, 2)
        .reshape(coefs, list_len * coefs)
    )
    column_vec = coarse_picked.transpose(1, 0).reshape(list_len * coefs, 1)
    coarse_local = jnp.dot(stacked, column_vec, preferred_element_type=jnp.float32).astype(
        jnp.bfloat16
    )
    downward = jnp.dot(down_shift[octant], coarse_local, preferred_element_type=jnp.float32).astype(
        jnp.bfloat16
    )
    for level in range(LOCAL_LEVELS - 1):
        downward = lower_level(downward, down_shift).astype(jnp.bfloat16)
    chain_part = lower_level(downward, down_shift)
    buffer = jnp.concatenate([multipoles, arrived], axis=1)
    far_total = far_field(buffer, far_shift, leaf_src, leaf_kind)
    return (chain_part + far_total).astype(jnp.bfloat16)


def solution(mesh):
    in_specs = (
        P(None, ("gx", "gy", "gz")),
        P(),
        P(),
        P(),
        P("gx", ("gy", "gz"), None, None),
        P(None, ("gx", "gy", "gz")),
        P(None, ("gx", "gy", "gz")),
        P(),
        P(),
    )
    out_specs = P(None, ("gx", "gy", "gz"))
    return jax.shard_map(
        on_device, mesh=mesh, in_specs=in_specs, out_specs=out_specs, check_vma=False
    )
```

```python
import jax
import jax.numpy as jnp
from jax import lax
from jax.experimental import pallas as pl
from jax.experimental.pallas import tpu as pltpu
from jax.sharding import PartitionSpec as P

LOCAL_LEVELS = 3
LANES = 384


def lift_level(children, up_shift):
    coefs = children.shape[0]
    count = children.shape[1] // 8
    child_stack = children.reshape(coefs, count, 8).transpose(2, 0, 1).reshape(8 * coefs, count)
    shift_table = up_shift.transpose(1, 0, 2).reshape(coefs, 8 * coefs)
    return jnp.dot(shift_table, child_stack, preferred_element_type=jnp.float32)


def lower_level(parent, down_shift):
    coefs = parent.shape[0]
    count = parent.shape[1]
    spread = jnp.dot(
        down_shift.reshape(8 * coefs, coefs), parent, preferred_element_type=jnp.float32
    )
    return spread.reshape(8, coefs, count).transpose(1, 2, 0).reshape(coefs, 8 * count)


def far_kernel(idx_ref, buf_ref, fs_ref, out_ref, table_ref):
    kinds = fs_ref.shape[0]
    rows = buf_ref.shape[0]
    for k in range(kinds):
        table_ref[pl.ds(k * rows, rows), :] = jnp.dot(
            buf_ref[...], fs_ref[k], preferred_element_type=jnp.float32
        )
    targets = out_ref.shape[0]
    lists = idx_ref.shape[0] // targets

    def body(t, carry):
        base = t * lists
        acc = table_ref[pl.ds(idx_ref[base], 1), :]
        for l in range(1, lists):
            acc = acc + table_ref[pl.ds(idx_ref[base + l], 1), :]
        out_ref[pl.ds(t, 1), :] = acc
        return carry

    lax.fori_loop(0, targets, body, 0)


def far_field(buffer, far_shift, leaf_src, leaf_kind):
    coefs, rows = buffer.shape
    kinds = far_shift.shape[0]
    lists, targets = leaf_src.shape
    pad = LANES - coefs
    buf_t = jnp.pad(buffer.T, ((0, 0), (0, pad)))
    fs_t = jnp.pad(far_shift.transpose(0, 2, 1), ((0, 0), (0, pad), (0, pad)))
    idx = (leaf_kind * rows + leaf_src).T.reshape(lists * targets)
    out = pl.pallas_call(
        far_kernel,
        out_shape=jax.ShapeDtypeStruct((targets, LANES), jnp.float32),
        in_specs=[
            pl.BlockSpec(memory_space=pltpu.SMEM),
            pl.BlockSpec(memory_space=pltpu.VMEM),
            pl.BlockSpec(memory_space=pltpu.VMEM),
        ],
        out_specs=pl.BlockSpec(memory_space=pltpu.VMEM),
        scratch_shapes=[pltpu.VMEM((kinds * rows, LANES), jnp.float32)],
    )(idx, buf_t, fs_t)
    return out[:, :coefs].T


def gather_columns(column_block, axes):
    group = lax.axis_size(axes)
    width = column_block.shape[1]
    spread = jnp.broadcast_to(column_block[:, None, :], (column_block.shape[0], group, width))
    spread = spread.reshape(column_block.shape[0], group * width)
    return lax.all_to_all(spread, axes, split_axis=1, concat_axis=1, tiled=True)


def on_device(
    multipoles,
    up_shift,
    down_shift,
    far_shift,
    send_list,
    leaf_src,
    leaf_kind,
    coarse_src,
    coarse_kind,
):
    coefs = multipoles.shape[0]
    flat_index = lax.axis_index(("gx", "gy", "gz"))
    coarse_box = flat_index // 8
    octant = flat_index % 8
    peer_count = lax.axis_size(("gy", "gz"))
    slot_count = send_list.shape[3]
    send_order = send_list.reshape(peer_count * slot_count)
    outgoing = jnp.take(multipoles, send_order, axis=1)
    arrived = lax.all_to_all(outgoing, ("gy", "gz"), split_axis=1, concat_axis=1, tiled=True)
    upward = multipoles
    for level in range(LOCAL_LEVELS):
        upward = lift_level(upward, up_shift).astype(jnp.bfloat16)
    row_boxes = gather_columns(upward, "gz")
    row_multi = lift_level(row_boxes, up_shift).astype(jnp.bfloat16)
    row_multi, arrived = lax.optimization_barrier((row_multi, arrived))
    coarse_multi = gather_columns(row_multi, ("gx", "gy"))
    coarse_cols = coarse_src[:, coarse_box]
    coarse_kinds = coarse_kind[:, coarse_box]
    list_len = coarse_cols.shape[0]
    coarse_picked = jnp.take(coarse_multi, coarse_cols, axis=1)
    stacked = (
        jnp.take(far_shift, coarse_kinds, axis=0)
        .transpose(1, 0, 2)
        .reshape(coefs, list_len * coefs)
    )
    column_vec = coarse_picked.transpose(1, 0).reshape(list_len * coefs, 1)
    coarse_local = jnp.dot(stacked, column_vec, preferred_element_type=jnp.float32).astype(
        jnp.bfloat16
    )
    downward = jnp.dot(down_shift[octant], coarse_local, preferred_element_type=jnp.float32).astype(
        jnp.bfloat16
    )
    for level in range(LOCAL_LEVELS - 1):
        downward = lower_level(downward, down_shift).astype(jnp.bfloat16)
    chain_part = lower_level(downward, down_shift)
    buffer = jnp.concatenate([multipoles, arrived], axis=1)
    far_total = far_field(buffer, far_shift, leaf_src, leaf_kind)
    return (chain_part + far_total).astype(jnp.bfloat16)


def solution(mesh):
    in_specs = (
        P(None, ("gx", "gy", "gz")),
        P(),
        P(),
        P(),
        P("gx", ("gy", "gz"), None, None),
        P(None, ("gx", "gy", "gz")),
        P(None, ("gx", "gy", "gz")),
        P(),
        P(),
    )
    out_specs = P(None, ("gx", "gy", "gz"))
    return jax.shard_map(
        on_device, mesh=mesh, in_specs=in_specs, out_specs=out_specs, check_vma=False
    )
```

```python
import jax
import jax.numpy as jnp
from jax import lax
from jax.experimental import pallas as pl
from jax.experimental.pallas import tpu as pltpu
from jax.sharding import PartitionSpec as P

LOCAL_LEVELS = 3
LANE = 128
CHUNKS = 3


def lift_level(children, up_shift):
    coefs = children.shape[0]
    count = children.shape[1] // 8
    child_stack = children.reshape(coefs, count, 8).transpose(2, 0, 1).reshape(8 * coefs, count)
    shift_table = up_shift.transpose(1, 0, 2).reshape(coefs, 8 * coefs)
    return jnp.dot(shift_table, child_stack, preferred_element_type=jnp.float32)


def lower_level(parent, down_shift):
    coefs = parent.shape[0]
    count = parent.shape[1]
    spread = jnp.dot(
        down_shift.reshape(8 * coefs, coefs), parent, preferred_element_type=jnp.float32
    )
    return spread.reshape(8, coefs, count).transpose(1, 2, 0).reshape(coefs, 8 * count)


def far_kernel(idx_ref, buf_ref, fs_ref, out_ref, table_ref):
    kinds = fs_ref.shape[0]
    rows = buf_ref.shape[0]
    for k in range(kinds):
        for j in range(CHUNKS):
            part = jnp.dot(
                buf_ref[...], fs_ref[k, :, pl.ds(j * LANE, LANE)], preferred_element_type=jnp.float32
            )
            table_ref[pl.ds(CHUNKS * k * rows + j, rows, stride=CHUNKS), :] = part
    targets = out_ref.shape[0] // CHUNKS
    lists = idx_ref.shape[0] // targets

    def body(t, carry):
        base = t * lists
        acc = table_ref[pl.ds(idx_ref[base], CHUNKS), :]
        for l in range(1, lists):
            acc = acc + table_ref[pl.ds(idx_ref[base + l], CHUNKS), :]
        out_ref[pl.ds(t * CHUNKS, CHUNKS), :] = acc
        return carry

    lax.fori_loop(0, targets, body, 0, unroll=8)


def far_field(buffer, far_shift, leaf_src, leaf_kind):
    coefs, rows = buffer.shape
    kinds = far_shift.shape[0]
    lists, targets = leaf_src.shape
    width = CHUNKS * LANE
    buf_t = jnp.pad(buffer.T, ((0, 0), (0, width - coefs)))
    fs_t = jnp.pad(far_shift.transpose(0, 2, 1), ((0, 0), (0, width - coefs), (0, width - coefs)))
    idx = (CHUNKS * (leaf_kind * rows + leaf_src)).T.reshape(lists * targets)
    out = pl.pallas_call(
        far_kernel,
        out_shape=jax.ShapeDtypeStruct((targets * CHUNKS, LANE), jnp.float32),
        in_specs=[
            pl.BlockSpec(memory_space=pltpu.SMEM),
            pl.BlockSpec(memory_space=pltpu.VMEM),
            pl.BlockSpec(memory_space=pltpu.VMEM),
        ],
        out_specs=pl.BlockSpec(memory_space=pltpu.VMEM),
        scratch_shapes=[pltpu.VMEM((kinds * rows * CHUNKS, LANE), jnp.float32)],
    )(idx, buf_t, fs_t)
    return out.reshape(targets, width)[:, :coefs].T


def gather_columns(column_block, axes):
    group = lax.axis_size(axes)
    width = column_block.shape[1]
    spread = jnp.broadcast_to(column_block[:, None, :], (column_block.shape[0], group, width))
    spread = spread.reshape(column_block.shape[0], group * width)
    return lax.all_to_all(spread, axes, split_axis=1, concat_axis=1, tiled=True)


def on_device(
    multipoles,
    up_shift,
    down_shift,
    far_shift,
    send_list,
    leaf_src,
    leaf_kind,
    coarse_src,
    coarse_kind,
):
    coefs = multipoles.shape[0]
    flat_index = lax.axis_index(("gx", "gy", "gz"))
    coarse_box = flat_index // 8
    octant = flat_index % 8
    peer_count = lax.axis_size(("gy", "gz"))
    slot_count = send_list.shape[3]
    send_order = send_list.reshape(peer_count * slot_count)
    outgoing = jnp.take(multipoles, send_order, axis=1)
    arrived = lax.all_to_all(outgoing, ("gy", "gz"), split_axis=1, concat_axis=1, tiled=True)
    upward = multipoles
    for level in range(LOCAL_LEVELS):
        upward = lift_level(upward, up_shift).astype(jnp.bfloat16)
    row_boxes = gather_columns(upward, "gz")
    row_multi = lift_level(row_boxes, up_shift).astype(jnp.bfloat16)
    coarse_multi = gather_columns(row_multi, ("gx", "gy"))
    coarse_cols = coarse_src[:, coarse_box]
    coarse_kinds = coarse_kind[:, coarse_box]
    list_len = coarse_cols.shape[0]
    coarse_picked = jnp.take(coarse_multi, coarse_cols, axis=1)
    stacked = (
        jnp.take(far_shift, coarse_kinds, axis=0)
        .transpose(1, 0, 2)
        .reshape(coefs, list_len * coefs)
    )
    column_vec = coarse_picked.transpose(1, 0).reshape(list_len * coefs, 1)
    coarse_local = jnp.dot(stacked, column_vec, preferred_element_type=jnp.float32).astype(
        jnp.bfloat16
    )
    downward = jnp.dot(down_shift[octant], coarse_local, preferred_element_type=jnp.float32).astype(
        jnp.bfloat16
    )
    for level in range(LOCAL_LEVELS - 1):
        downward = lower_level(downward, down_shift).astype(jnp.bfloat16)
    chain_part = lower_level(downward, down_shift)
    buffer = jnp.concatenate([multipoles, arrived], axis=1)
    far_total = far_field(buffer, far_shift, leaf_src, leaf_kind)
    return (chain_part + far_total).astype(jnp.bfloat16)


def solution(mesh):
    in_specs = (
        P(None, ("gx", "gy", "gz")),
        P(),
        P(),
        P(),
        P("gx", ("gy", "gz"), None, None),
        P(None, ("gx", "gy", "gz")),
        P(None, ("gx", "gy", "gz")),
        P(),
        P(),
    )
    out_specs = P(None, ("gx", "gy", "gz"))
    return jax.shard_map(
        on_device, mesh=mesh, in_specs=in_specs, out_specs=out_specs, check_vma=False
    )
```

```python
import jax
import jax.numpy as jnp
from jax import lax
from jax.experimental import pallas as pl
from jax.experimental.pallas import tpu as pltpu
from jax.sharding import PartitionSpec as P

LOCAL_LEVELS = 3
LANE = 128
CHUNKS = 3


def lift_level(children, up_shift):
    coefs = children.shape[0]
    count = children.shape[1] // 8
    child_stack = children.reshape(coefs, count, 8).transpose(2, 0, 1)
    per_octant = lax.dot_general(
        up_shift, child_stack, (((2,), (1,)), ((0,), (0,))), preferred_element_type=jnp.float32
    )
    return per_octant.sum(axis=0)


def lower_level(parent, down_shift):
    coefs = parent.shape[0]
    count = parent.shape[1]
    spread = jnp.dot(
        down_shift.reshape(8 * coefs, coefs), parent, preferred_element_type=jnp.float32
    )
    return spread.reshape(8, coefs, count).transpose(1, 2, 0).reshape(coefs, 8 * count)


def far_kernel(idx_ref, buf_ref, fs_ref, out_ref, table_ref):
    kinds = fs_ref.shape[0]
    rows = buf_ref.shape[0]
    for k in range(kinds):
        for j in range(CHUNKS):
            part = jnp.dot(
                buf_ref[...], fs_ref[k, :, pl.ds(j * LANE, LANE)], preferred_element_type=jnp.float32
            )
            table_ref[pl.ds(CHUNKS * k * rows + j, rows, stride=CHUNKS), :] = part
    targets = out_ref.shape[0] // CHUNKS
    lists = idx_ref.shape[0] // targets

    def body(t, carry):
        base = t * lists
        acc = table_ref[pl.ds(idx_ref[base], CHUNKS), :]
        for l in range(1, lists):
            acc = acc + table_ref[pl.ds(idx_ref[base + l], CHUNKS), :]
        out_ref[pl.ds(t * CHUNKS, CHUNKS), :] = acc
        return carry

    lax.fori_loop(0, targets, body, 0, unroll=8)


def far_field(buffer, far_shift, leaf_src, leaf_kind):
    coefs, rows = buffer.shape
    kinds = far_shift.shape[0]
    lists, targets = leaf_src.shape
    width = CHUNKS * LANE
    buf_t = jnp.pad(buffer.T, ((0, 0), (0, width - coefs)))
    fs_t = jnp.pad(far_shift.transpose(0, 2, 1), ((0, 0), (0, width - coefs), (0, width - coefs)))
    idx = (CHUNKS * (leaf_kind * rows + leaf_src)).T.reshape(lists * targets)
    out = pl.pallas_call(
        far_kernel,
        out_shape=jax.ShapeDtypeStruct((targets * CHUNKS, LANE), jnp.float32),
        in_specs=[
            pl.BlockSpec(memory_space=pltpu.SMEM),
            pl.BlockSpec(memory_space=pltpu.VMEM),
            pl.BlockSpec(memory_space=pltpu.VMEM),
        ],
        out_specs=pl.BlockSpec(memory_space=pltpu.VMEM),
        scratch_shapes=[pltpu.VMEM((kinds * rows * CHUNKS, LANE), jnp.float32)],
    )(idx, buf_t, fs_t)
    return out.reshape(targets, width)[:, :coefs].T


def gather_columns(column_block, axes):
    group = lax.axis_size(axes)
    width = column_block.shape[1]
    spread = jnp.broadcast_to(column_block[:, None, :], (column_block.shape[0], group, width))
    spread = spread.reshape(column_block.shape[0], group * width)
    return lax.all_to_all(spread, axes, split_axis=1, concat_axis=1, tiled=True)


def on_device(
    multipoles,
    up_shift,
    down_shift,
    far_shift,
    send_list,
    leaf_src,
    leaf_kind,
    coarse_src,
    coarse_kind,
):
    coefs = multipoles.shape[0]
    flat_index = lax.axis_index(("gx", "gy", "gz"))
    coarse_box = flat_index // 8
    octant = flat_index % 8
    peer_count = lax.axis_size(("gy", "gz"))
    slot_count = send_list.shape[3]
    send_order = send_list.reshape(peer_count * slot_count)
    outgoing = jnp.take(multipoles, send_order, axis=1)
    arrived = lax.all_to_all(outgoing, ("gy", "gz"), split_axis=1, concat_axis=1, tiled=True)
    upward = multipoles
    for level in range(LOCAL_LEVELS):
        upward = lift_level(upward, up_shift).astype(jnp.bfloat16)
    row_boxes = gather_columns(upward, "gz")
    row_multi = lift_level(row_boxes, up_shift).astype(jnp.bfloat16)
    coarse_multi = gather_columns(row_multi, ("gx", "gy"))
    coarse_cols = coarse_src[:, coarse_box]
    coarse_kinds = coarse_kind[:, coarse_box]
    list_len = coarse_cols.shape[0]
    coarse_picked = jnp.take(coarse_multi, coarse_cols, axis=1)
    stacked = (
        jnp.take(far_shift, coarse_kinds, axis=0)
        .transpose(1, 0, 2)
        .reshape(coefs, list_len * coefs)
    )
    column_vec = coarse_picked.transpose(1, 0).reshape(list_len * coefs, 1)
    coarse_local = jnp.dot(stacked, column_vec, preferred_element_type=jnp.float32).astype(
        jnp.bfloat16
    )
    downward = jnp.dot(down_shift[octant], coarse_local, preferred_element_type=jnp.float32).astype(
        jnp.bfloat16
    )
    for level in range(LOCAL_LEVELS - 1):
        downward = lower_level(downward, down_shift).astype(jnp.bfloat16)
    chain_part = lower_level(downward, down_shift)
    buffer = jnp.concatenate([multipoles, arrived], axis=1)
    far_total = far_field(buffer, far_shift, leaf_src, leaf_kind)
    return (chain_part + far_total).astype(jnp.bfloat16)


def solution(mesh):
    in_specs = (
        P(None, ("gx", "gy", "gz")),
        P(),
        P(),
        P(),
        P("gx", ("gy", "gz"), None, None),
        P(None, ("gx", "gy", "gz")),
        P(None, ("gx", "gy", "gz")),
        P(),
        P(),
    )
    out_specs = P(None, ("gx", "gy", "gz"))
    return jax.shard_map(
        on_device, mesh=mesh, in_specs=in_specs, out_specs=out_specs, check_vma=False
    )
```

```python
import jax
import jax.numpy as jnp
from jax import lax
from jax.experimental import pallas as pl
from jax.experimental.pallas import tpu as pltpu
from jax.sharding import PartitionSpec as P

LOCAL_LEVELS = 3
LANE = 128
CHUNKS = 3


def lift_level(children, up_shift):
    coefs = children.shape[0]
    count = children.shape[1] // 8
    child_stack = children.reshape(coefs, count, 8).transpose(2, 0, 1)
    per_octant = lax.dot_general(
        up_shift, child_stack, (((2,), (1,)), ((0,), (0,))), preferred_element_type=jnp.float32
    )
    return per_octant.sum(axis=0)


def lower_level(parent, down_shift):
    coefs = parent.shape[0]
    count = parent.shape[1]
    spread = jnp.dot(
        down_shift.reshape(8 * coefs, coefs), parent, preferred_element_type=jnp.float32
    )
    return spread.reshape(8, coefs, count).transpose(1, 2, 0).reshape(coefs, 8 * count)


def far_kernel(idx_ref, buf_ref, fs_ref, out_ref, table_ref, acc_ref):
    kinds = fs_ref.shape[0]
    rows = buf_ref.shape[0]
    for k in range(kinds):
        for j in range(CHUNKS):
            part = jnp.dot(
                buf_ref[...], fs_ref[k, :, pl.ds(j * LANE, LANE)], preferred_element_type=jnp.float32
            )
            table_ref[pl.ds(CHUNKS * k * rows + j, rows, stride=CHUNKS), :] = part
    targets = out_ref.shape[1]
    lists = idx_ref.shape[0] // targets

    def body(t, carry):
        base = t * lists
        acc = table_ref[pl.ds(idx_ref[base], CHUNKS), :]
        for l in range(1, lists):
            acc = acc + table_ref[pl.ds(idx_ref[base + l], CHUNKS), :]
        acc_ref[pl.ds(t * CHUNKS, CHUNKS), :] = acc
        return carry

    lax.fori_loop(0, targets, body, 0, unroll=8)
    for j in range(CHUNKS):
        out_ref[pl.ds(j * LANE, LANE), :] = acc_ref[pl.ds(j, targets, stride=CHUNKS), :].T


def far_field(buffer, far_shift, leaf_src, leaf_kind):
    coefs, rows = buffer.shape
    kinds = far_shift.shape[0]
    lists, targets = leaf_src.shape
    width = CHUNKS * LANE
    buf_t = jnp.pad(buffer.T, ((0, 0), (0, width - coefs)))
    fs_t = jnp.pad(far_shift.transpose(0, 2, 1), ((0, 0), (0, width - coefs), (0, width - coefs)))
    idx = (CHUNKS * (leaf_kind * rows + leaf_src)).T.reshape(lists * targets)
    out = pl.pallas_call(
        far_kernel,
        out_shape=jax.ShapeDtypeStruct((width, targets), jnp.float32),
        in_specs=[
            pl.BlockSpec(memory_space=pltpu.SMEM),
            pl.BlockSpec(memory_space=pltpu.VMEM),
            pl.BlockSpec(memory_space=pltpu.VMEM),
        ],
        out_specs=pl.BlockSpec(memory_space=pltpu.VMEM),
        scratch_shapes=[
            pltpu.VMEM((kinds * rows * CHUNKS, LANE), jnp.float32),
            pltpu.VMEM((targets * CHUNKS, LANE), jnp.float32),
        ],
    )(idx, buf_t, fs_t)
    return out[:coefs, :]


def gather_columns(column_block, axes):
    group = lax.axis_size(axes)
    width = column_block.shape[1]
    spread = jnp.broadcast_to(column_block[:, None, :], (column_block.shape[0], group, width))
    spread = spread.reshape(column_block.shape[0], group * width)
    return lax.all_to_all(spread, axes, split_axis=1, concat_axis=1, tiled=True)


def on_device(
    multipoles,
    up_shift,
    down_shift,
    far_shift,
    send_list,
    leaf_src,
    leaf_kind,
    coarse_src,
    coarse_kind,
):
    coefs = multipoles.shape[0]
    flat_index = lax.axis_index(("gx", "gy", "gz"))
    coarse_box = flat_index // 8
    octant = flat_index % 8
    peer_count = lax.axis_size(("gy", "gz"))
    slot_count = send_list.shape[3]
    send_order = send_list.reshape(peer_count * slot_count)
    outgoing = jnp.take(multipoles, send_order, axis=1)
    arrived = lax.all_to_all(outgoing, ("gy", "gz"), split_axis=1, concat_axis=1, tiled=True)
    upward = multipoles
    for level in range(LOCAL_LEVELS):
        upward = lift_level(upward, up_shift).astype(jnp.bfloat16)
    row_boxes = gather_columns(upward, "gz")
    row_multi = lift_level(row_boxes, up_shift).astype(jnp.bfloat16)
    coarse_multi = gather_columns(row_multi, ("gx", "gy"))
    coarse_cols = coarse_src[:, coarse_box]
    coarse_kinds = coarse_kind[:, coarse_box]
    list_len = coarse_cols.shape[0]
    coarse_picked = jnp.take(coarse_multi, coarse_cols, axis=1)
    stacked = (
        jnp.take(far_shift, coarse_kinds, axis=0)
        .transpose(1, 0, 2)
        .reshape(coefs, list_len * coefs)
    )
    column_vec = coarse_picked.transpose(1, 0).reshape(list_len * coefs, 1)
    coarse_local = jnp.dot(stacked, column_vec, preferred_element_type=jnp.float32).astype(
        jnp.bfloat16
    )
    downward = jnp.dot(down_shift[octant], coarse_local, preferred_element_type=jnp.float32).astype(
        jnp.bfloat16
    )
    for level in range(LOCAL_LEVELS - 1):
        downward = lower_level(downward, down_shift).astype(jnp.bfloat16)
    chain_part = lower_level(downward, down_shift)
    buffer = jnp.concatenate([multipoles, arrived], axis=1)
    far_total = far_field(buffer, far_shift, leaf_src, leaf_kind)
    return (chain_part + far_total).astype(jnp.bfloat16)


def solution(mesh):
    in_specs = (
        P(None, ("gx", "gy", "gz")),
        P(),
        P(),
        P(),
        P("gx", ("gy", "gz"), None, None),
        P(None, ("gx", "gy", "gz")),
        P(None, ("gx", "gy", "gz")),
        P(),
        P(),
    )
    out_specs = P(None, ("gx", "gy", "gz"))
    return jax.shard_map(
        on_device, mesh=mesh, in_specs=in_specs, out_specs=out_specs, check_vma=False
    )
```

```python
import jax
import jax.numpy as jnp
from jax import lax
from jax.experimental import pallas as pl
from jax.experimental.pallas import tpu as pltpu
from jax.sharding import PartitionSpec as P

LOCAL_LEVELS = 3
LANE = 128
CHUNKS = 3


def lift_level(children, up_shift):
    coefs = children.shape[0]
    count = children.shape[1] // 8
    child_stack = children.reshape(coefs, count, 8).transpose(2, 0, 1)
    per_octant = lax.dot_general(
        up_shift, child_stack, (((2,), (1,)), ((0,), (0,))), preferred_element_type=jnp.float32
    )
    return per_octant.sum(axis=0)


def lower_level(parent, down_shift):
    coefs = parent.shape[0]
    count = parent.shape[1]
    spread = jnp.dot(
        down_shift.reshape(8 * coefs, coefs), parent, preferred_element_type=jnp.float32
    )
    return spread.reshape(8, coefs, count).transpose(1, 2, 0).reshape(coefs, 8 * count)


def far_kernel(idx_ref, buf_ref, fs_ref, out_ref, table_ref, acc_ref):
    kinds = fs_ref.shape[0]
    rows = buf_ref.shape[0]
    for k in range(kinds):
        whole = jnp.dot(buf_ref[...], fs_ref[k], preferred_element_type=jnp.float32)
        for j in range(CHUNKS):
            table_ref[pl.ds(CHUNKS * k * rows + j, rows, stride=CHUNKS), :] = whole[
                :, j * LANE : (j + 1) * LANE
            ]
    targets = out_ref.shape[1]
    lists = idx_ref.shape[0] // targets

    def body(t, carry):
        base = t * lists
        acc = table_ref[pl.ds(idx_ref[base], CHUNKS), :]
        for l in range(1, lists):
            acc = acc + table_ref[pl.ds(idx_ref[base + l], CHUNKS), :]
        acc_ref[pl.ds(t * CHUNKS, CHUNKS), :] = acc
        return carry

    lax.fori_loop(0, targets, body, 0, unroll=8)
    for j in range(CHUNKS):
        out_ref[pl.ds(j * LANE, LANE), :] = acc_ref[pl.ds(j, targets, stride=CHUNKS), :].T


def far_field(buffer, far_shift, leaf_src, leaf_kind):
    coefs, rows = buffer.shape
    kinds = far_shift.shape[0]
    lists, targets = leaf_src.shape
    width = CHUNKS * LANE
    buf_t = jnp.pad(buffer.T, ((0, 0), (0, width - coefs)))
    fs_t = jnp.pad(far_shift.transpose(0, 2, 1), ((0, 0), (0, width - coefs), (0, width - coefs)))
    idx = (CHUNKS * (leaf_kind * rows + leaf_src)).T.reshape(lists * targets)
    out = pl.pallas_call(
        far_kernel,
        out_shape=jax.ShapeDtypeStruct((width, targets), jnp.float32),
        in_specs=[
            pl.BlockSpec(memory_space=pltpu.SMEM),
            pl.BlockSpec(memory_space=pltpu.VMEM),
            pl.BlockSpec(memory_space=pltpu.VMEM),
        ],
        out_specs=pl.BlockSpec(memory_space=pltpu.VMEM),
        scratch_shapes=[
            pltpu.VMEM((kinds * rows * CHUNKS, LANE), jnp.float32),
            pltpu.VMEM((targets * CHUNKS, LANE), jnp.float32),
        ],
    )(idx, buf_t, fs_t)
    return out[:coefs, :]


def gather_columns(column_block, axes):
    group = lax.axis_size(axes)
    width = column_block.shape[1]
    spread = jnp.broadcast_to(column_block[:, None, :], (column_block.shape[0], group, width))
    spread = spread.reshape(column_block.shape[0], group * width)
    return lax.all_to_all(spread, axes, split_axis=1, concat_axis=1, tiled=True)


def on_device(
    multipoles,
    up_shift,
    down_shift,
    far_shift,
    send_list,
    leaf_src,
    leaf_kind,
    coarse_src,
    coarse_kind,
):
    coefs = multipoles.shape[0]
    flat_index = lax.axis_index(("gx", "gy", "gz"))
    coarse_box = flat_index // 8
    octant = flat_index % 8
    peer_count = lax.axis_size(("gy", "gz"))
    slot_count = send_list.shape[3]
    send_order = send_list.reshape(peer_count * slot_count)
    outgoing = jnp.take(multipoles, send_order, axis=1)
    arrived = lax.all_to_all(outgoing, ("gy", "gz"), split_axis=1, concat_axis=1, tiled=True)
    upward = multipoles
    for level in range(LOCAL_LEVELS):
        upward = lift_level(upward, up_shift).astype(jnp.bfloat16)
    row_boxes = gather_columns(upward, "gz")
    row_multi = lift_level(row_boxes, up_shift).astype(jnp.bfloat16)
    coarse_multi = gather_columns(row_multi, ("gx", "gy"))
    coarse_cols = coarse_src[:, coarse_box]
    coarse_kinds = coarse_kind[:, coarse_box]
    list_len = coarse_cols.shape[0]
    coarse_picked = jnp.take(coarse_multi, coarse_cols, axis=1)
    stacked = (
        jnp.take(far_shift, coarse_kinds, axis=0)
        .transpose(1, 0, 2)
        .reshape(coefs, list_len * coefs)
    )
    column_vec = coarse_picked.transpose(1, 0).reshape(list_len * coefs, 1)
    coarse_local = jnp.dot(stacked, column_vec, preferred_element_type=jnp.float32).astype(
        jnp.bfloat16
    )
    downward = jnp.dot(down_shift[octant], coarse_local, preferred_element_type=jnp.float32).astype(
        jnp.bfloat16
    )
    for level in range(LOCAL_LEVELS - 1):
        downward = lower_level(downward, down_shift).astype(jnp.bfloat16)
    chain_part = lower_level(downward, down_shift)
    buffer = jnp.concatenate([multipoles, arrived], axis=1)
    far_total = far_field(buffer, far_shift, leaf_src, leaf_kind)
    return (chain_part + far_total).astype(jnp.bfloat16)


def solution(mesh):
    in_specs = (
        P(None, ("gx", "gy", "gz")),
        P(),
        P(),
        P(),
        P("gx", ("gy", "gz"), None, None),
        P(None, ("gx", "gy", "gz")),
        P(None, ("gx", "gy", "gz")),
        P(),
        P(),
    )
    out_specs = P(None, ("gx", "gy", "gz"))
    return jax.shard_map(
        on_device, mesh=mesh, in_specs=in_specs, out_specs=out_specs, check_vma=False
    )
```

```python
import jax
import jax.numpy as jnp
from jax import lax
from jax.experimental import pallas as pl
from jax.experimental.pallas import tpu as pltpu
from jax.sharding import PartitionSpec as P

LOCAL_LEVELS = 3
LANE = 128
CHUNKS = 3


def lift_level(children, up_shift):
    coefs = children.shape[0]
    count = children.shape[1] // 8
    child_stack = children.reshape(coefs, count, 8).transpose(2, 0, 1)
    per_octant = lax.dot_general(
        up_shift, child_stack, (((2,), (1,)), ((0,), (0,))), preferred_element_type=jnp.float32
    )
    return per_octant.sum(axis=0)


def lower_level(parent, down_shift):
    coefs = parent.shape[0]
    count = parent.shape[1]
    spread = jnp.dot(
        down_shift.reshape(8 * coefs, coefs), parent, preferred_element_type=jnp.float32
    )
    return spread.reshape(8, coefs, count).transpose(1, 2, 0).reshape(coefs, 8 * count)


def far_kernel(idx_ref, own_ref, arr_ref, fs_ref, out_ref, table_ref, acc_ref):
    kinds = fs_ref.shape[0]
    own = own_ref.shape[0]
    rows = own + arr_ref.shape[0]
    for k in range(kinds):
        for src_ref, first in ((own_ref, 0), (arr_ref, own)):
            whole = jnp.dot(src_ref[...], fs_ref[k], preferred_element_type=jnp.float32)
            for j in range(CHUNKS):
                table_ref[
                    pl.ds(CHUNKS * (k * rows + first) + j, src_ref.shape[0], stride=CHUNKS), :
                ] = whole[:, j * LANE : (j + 1) * LANE]
    targets = out_ref.shape[1]
    lists = idx_ref.shape[0] // targets

    def body(t, carry):
        base = t * lists
        acc = table_ref[pl.ds(idx_ref[base], CHUNKS), :]
        for l in range(1, lists):
            acc = acc + table_ref[pl.ds(idx_ref[base + l], CHUNKS), :]
        acc_ref[pl.ds(t * CHUNKS, CHUNKS), :] = acc
        return carry

    lax.fori_loop(0, targets, body, 0, unroll=8)
    for j in range(CHUNKS):
        out_ref[pl.ds(j * LANE, LANE), :] = acc_ref[pl.ds(j, targets, stride=CHUNKS), :].T


def far_field(own_rows, arrived_rows, far_shift, leaf_src, leaf_kind):
    rows = own_rows.shape[0] + arrived_rows.shape[0]
    coefs = own_rows.shape[1]
    kinds = far_shift.shape[0]
    lists, targets = leaf_src.shape
    width = CHUNKS * LANE
    fs_t = jnp.pad(far_shift.transpose(0, 2, 1), ((0, 0), (0, 0), (0, width - coefs)))
    idx = (CHUNKS * (leaf_kind * rows + leaf_src)).T.reshape(lists * targets)
    vmem = pl.BlockSpec(memory_space=pltpu.VMEM)
    out = pl.pallas_call(
        far_kernel,
        out_shape=jax.ShapeDtypeStruct((width, targets), jnp.float32),
        in_specs=[pl.BlockSpec(memory_space=pltpu.SMEM), vmem, vmem, vmem],
        out_specs=vmem,
        scratch_shapes=[
            pltpu.VMEM((kinds * rows * CHUNKS, LANE), jnp.float32),
            pltpu.VMEM((targets * CHUNKS, LANE), jnp.float32),
        ],
    )(idx, own_rows, arrived_rows, fs_t)
    return out[:coefs, :]


def gather_columns(column_block, axes):
    group = lax.axis_size(axes)
    width = column_block.shape[1]
    spread = jnp.broadcast_to(column_block[:, None, :], (column_block.shape[0], group, width))
    spread = spread.reshape(column_block.shape[0], group * width)
    return lax.all_to_all(spread, axes, split_axis=1, concat_axis=1, tiled=True)


def on_device(
    multipoles,
    up_shift,
    down_shift,
    far_shift,
    send_list,
    leaf_src,
    leaf_kind,
    coarse_src,
    coarse_kind,
):
    coefs = multipoles.shape[0]
    flat_index = lax.axis_index(("gx", "gy", "gz"))
    coarse_box = flat_index // 8
    octant = flat_index % 8
    peer_count = lax.axis_size(("gy", "gz"))
    slot_count = send_list.shape[3]
    send_order = send_list.reshape(peer_count * slot_count)
    own_rows = multipoles.T
    outgoing = jnp.take(own_rows, send_order, axis=0)
    arrived_rows = lax.all_to_all(outgoing, ("gy", "gz"), split_axis=0, concat_axis=0, tiled=True)
    upward = multipoles
    for level in range(LOCAL_LEVELS):
        upward = lift_level(upward, up_shift).astype(jnp.bfloat16)
    row_boxes = gather_columns(upward, "gz")
    row_multi = lift_level(row_boxes, up_shift).astype(jnp.bfloat16)
    coarse_multi = gather_columns(row_multi, ("gx", "gy"))
    coarse_cols = coarse_src[:, coarse_box]
    coarse_kinds = coarse_kind[:, coarse_box]
    list_len = coarse_cols.shape[0]
    coarse_picked = jnp.take(coarse_multi, coarse_cols, axis=1)
    stacked = (
        jnp.take(far_shift, coarse_kinds, axis=0)
        .transpose(1, 0, 2)
        .reshape(coefs, list_len * coefs)
    )
    column_vec = coarse_picked.transpose(1, 0).reshape(list_len * coefs, 1)
    coarse_local = jnp.dot(stacked, column_vec, preferred_element_type=jnp.float32).astype(
        jnp.bfloat16
    )
    downward = jnp.dot(down_shift[octant], coarse_local, preferred_element_type=jnp.float32).astype(
        jnp.bfloat16
    )
    for level in range(LOCAL_LEVELS - 1):
        downward = lower_level(downward, down_shift).astype(jnp.bfloat16)
    chain_part = lower_level(downward, down_shift)
    far_total = far_field(own_rows, arrived_rows, far_shift, leaf_src, leaf_kind)
    return (chain_part + far_total).astype(jnp.bfloat16)


def solution(mesh):
    in_specs = (
        P(None, ("gx", "gy", "gz")),
        P(),
        P(),
        P(),
        P("gx", ("gy", "gz"), None, None),
        P(None, ("gx", "gy", "gz")),
        P(None, ("gx", "gy", "gz")),
        P(),
        P(),
    )
    out_specs = P(None, ("gx", "gy", "gz"))
    return jax.shard_map(
        on_device, mesh=mesh, in_specs=in_specs, out_specs=out_specs, check_vma=False
    )
```

```python
import jax
import jax.numpy as jnp
from jax import lax
from jax.experimental import pallas as pl
from jax.experimental.pallas import tpu as pltpu
from jax.sharding import PartitionSpec as P

LOCAL_LEVELS = 3
LANE = 128
CHUNKS = 3


def lift_level(children, up_shift):
    coefs = children.shape[0]
    count = children.shape[1] // 8
    child_stack = children.reshape(coefs, count, 8).transpose(2, 0, 1)
    per_octant = lax.dot_general(
        up_shift, child_stack, (((2,), (1,)), ((0,), (0,))), preferred_element_type=jnp.float32
    )
    return per_octant.sum(axis=0)


def lower_level(parent, down_shift):
    coefs = parent.shape[0]
    count = parent.shape[1]
    spread = jnp.dot(
        down_shift.reshape(8 * coefs, coefs), parent, preferred_element_type=jnp.float32
    )
    return spread.reshape(8, coefs, count).transpose(1, 2, 0).reshape(coefs, 8 * count)


def far_kernel(idx_ref, buf_ref, fs_ref, out_ref, table_ref, acc_ref):
    kinds = fs_ref.shape[0]
    rows = buf_ref.shape[0]
    for k in range(kinds):
        whole = jnp.dot(buf_ref[...], fs_ref[k], preferred_element_type=jnp.float32)
        for j in range(CHUNKS):
            table_ref[pl.ds(CHUNKS * k * rows + j, rows, stride=CHUNKS), :] = whole[
                :, j * LANE : (j + 1) * LANE
            ]
    targets = out_ref.shape[1]
    lists = idx_ref.shape[0] // targets

    def body(t, carry):
        base = t * lists
        acc = table_ref[pl.ds(idx_ref[base], CHUNKS), :]
        for l in range(1, lists):
            acc = acc + table_ref[pl.ds(idx_ref[base + l], CHUNKS), :]
        acc_ref[pl.ds(t * CHUNKS, CHUNKS), :] = acc
        return carry

    lax.fori_loop(0, targets, body, 0, unroll=8)
    for j in range(CHUNKS):
        out_ref[pl.ds(j * LANE, LANE), :] = acc_ref[pl.ds(j, targets, stride=CHUNKS), :].T


def far_field(buffer, far_shift, leaf_src, leaf_kind):
    coefs, rows = buffer.shape
    kinds = far_shift.shape[0]
    lists, targets = leaf_src.shape
    width = CHUNKS * LANE
    buf_t = jnp.pad(buffer.T, ((0, 0), (0, width - coefs)))
    fs_t = jnp.pad(far_shift.transpose(0, 2, 1), ((0, 0), (0, width - coefs), (0, width - coefs)))
    idx = (CHUNKS * (leaf_kind * rows + leaf_src)).T.reshape(lists * targets)
    out = pl.pallas_call(
        far_kernel,
        out_shape=jax.ShapeDtypeStruct((width, targets), jnp.float32),
        in_specs=[
            pl.BlockSpec(memory_space=pltpu.SMEM),
            pl.BlockSpec(memory_space=pltpu.VMEM),
            pl.BlockSpec(memory_space=pltpu.VMEM),
        ],
        out_specs=pl.BlockSpec(memory_space=pltpu.VMEM),
        scratch_shapes=[
            pltpu.VMEM((kinds * rows * CHUNKS, LANE), jnp.float32),
            pltpu.VMEM((targets * CHUNKS, LANE), jnp.float32),
        ],
    )(idx, buf_t, fs_t)
    return out[:coefs, :]


def gather_columns(column_block, axes):
    group = lax.axis_size(axes)
    width = column_block.shape[1]
    spread = jnp.broadcast_to(column_block[:, None, :], (column_block.shape[0], group, width))
    spread = spread.reshape(column_block.shape[0], group * width)
    return lax.all_to_all(spread, axes, split_axis=1, concat_axis=1, tiled=True)


def on_device(
    multipoles,
    up_shift,
    down_shift,
    far_shift,
    send_list,
    leaf_src,
    leaf_kind,
    coarse_src,
    coarse_kind,
):
    coefs = multipoles.shape[0]
    flat_index = lax.axis_index(("gx", "gy", "gz"))
    coarse_box = flat_index // 8
    octant = flat_index % 8
    peer_count = lax.axis_size(("gy", "gz"))
    slot_count = send_list.shape[3]
    send_order = send_list.reshape(peer_count * slot_count)
    outgoing = jnp.take(multipoles, send_order, axis=1)
    arrived = lax.all_to_all(outgoing, ("gy", "gz"), split_axis=1, concat_axis=1, tiled=True)
    upward = multipoles
    for level in range(LOCAL_LEVELS):
        upward = lift_level(upward, up_shift).astype(jnp.bfloat16)
    slice_boxes = gather_columns(upward, ("gy", "gz"))
    slice_multi = lift_level(slice_boxes, up_shift).astype(jnp.bfloat16)
    coarse_multi = gather_columns(slice_multi, "gx")
    coarse_cols = coarse_src[:, coarse_box]
    coarse_kinds = coarse_kind[:, coarse_box]
    list_len = coarse_cols.shape[0]
    coarse_picked = jnp.take(coarse_multi, coarse_cols, axis=1)
    stacked = (
        jnp.take(far_shift, coarse_kinds, axis=0)
        .transpose(1, 0, 2)
        .reshape(coefs, list_len * coefs)
    )
    column_vec = coarse_picked.transpose(1, 0).reshape(list_len * coefs, 1)
    coarse_local = jnp.dot(stacked, column_vec, preferred_element_type=jnp.float32).astype(
        jnp.bfloat16
    )
    downward = jnp.dot(down_shift[octant], coarse_local, preferred_element_type=jnp.float32).astype(
        jnp.bfloat16
    )
    for level in range(LOCAL_LEVELS - 1):
        downward = lower_level(downward, down_shift).astype(jnp.bfloat16)
    chain_part = lower_level(downward, down_shift)
    buffer = jnp.concatenate([multipoles, arrived], axis=1)
    far_total = far_field(buffer, far_shift, leaf_src, leaf_kind)
    return (chain_part + far_total).astype(jnp.bfloat16)


def solution(mesh):
    in_specs = (
        P(None, ("gx", "gy", "gz")),
        P(),
        P(),
        P(),
        P("gx", ("gy", "gz"), None, None),
        P(None, ("gx", "gy", "gz")),
        P(None, ("gx", "gy", "gz")),
        P(),
        P(),
    )
    out_specs = P(None, ("gx", "gy", "gz"))
    return jax.shard_map(
        on_device, mesh=mesh, in_specs=in_specs, out_specs=out_specs, check_vma=False
    )
```

```python
import jax
import jax.numpy as jnp
from jax import lax
from jax.experimental import pallas as pl
from jax.experimental.pallas import tpu as pltpu
from jax.sharding import PartitionSpec as P

LOCAL_LEVELS = 3
LANE = 128
CHUNKS = 3


def lift_level(children, up_shift):
    coefs = children.shape[0]
    count = children.shape[1] // 8
    child_stack = children.reshape(coefs, count, 8).transpose(2, 0, 1)
    per_octant = lax.dot_general(
        up_shift, child_stack, (((2,), (1,)), ((0,), (0,))), preferred_element_type=jnp.float32
    )
    return per_octant.sum(axis=0)


def lower_level(parent, down_shift):
    coefs = parent.shape[0]
    count = parent.shape[1]
    spread = jnp.dot(
        down_shift.reshape(8 * coefs, coefs), parent, preferred_element_type=jnp.float32
    )
    return spread.reshape(8, coefs, count).transpose(1, 2, 0).reshape(coefs, 8 * count)


def far_kernel(idx_ref, buf_ref, fs_ref, chain_ref, out_ref, table_ref, acc_ref):
    kinds = fs_ref.shape[0]
    rows = buf_ref.shape[0]
    for k in range(kinds):
        whole = jnp.dot(buf_ref[...], fs_ref[k], preferred_element_type=jnp.float32)
        for j in range(CHUNKS):
            table_ref[pl.ds(CHUNKS * k * rows + j, rows, stride=CHUNKS), :] = whole[
                :, j * LANE : (j + 1) * LANE
            ]
    targets = out_ref.shape[1]
    lists = idx_ref.shape[0] // targets

    def body(t, carry):
        base = t * lists
        acc = table_ref[pl.ds(idx_ref[base], CHUNKS), :]
        for l in range(1, lists):
            acc = acc + table_ref[pl.ds(idx_ref[base + l], CHUNKS), :]
        acc_ref[pl.ds(t * CHUNKS, CHUNKS), :] = acc
        return carry

    lax.fori_loop(0, targets, body, 0, unroll=8)
    coefs = out_ref.shape[0]
    for j in range(CHUNKS):
        block = acc_ref[pl.ds(j, targets, stride=CHUNKS), :].T
        used = min(LANE, coefs - j * LANE)
        near = chain_ref[pl.ds(j * LANE, used), :]
        out_ref[pl.ds(j * LANE, used), :] = (block[:used] + near).astype(out_ref.dtype)


def far_field(buffer, far_shift, leaf_src, leaf_kind, chain_part):
    coefs, rows = buffer.shape
    kinds = far_shift.shape[0]
    lists, targets = leaf_src.shape
    width = CHUNKS * LANE
    buf_t = jnp.pad(buffer.T, ((0, 0), (0, width - coefs)))
    fs_t = jnp.pad(far_shift.transpose(0, 2, 1), ((0, 0), (0, width - coefs), (0, width - coefs)))
    idx = (CHUNKS * (leaf_kind * rows + leaf_src)).T.reshape(lists * targets)
    out = pl.pallas_call(
        far_kernel,
        out_shape=jax.ShapeDtypeStruct((coefs, targets), jnp.bfloat16),
        in_specs=[
            pl.BlockSpec(memory_space=pltpu.SMEM),
            pl.BlockSpec(memory_space=pltpu.VMEM),
            pl.BlockSpec(memory_space=pltpu.VMEM),
            pl.BlockSpec(memory_space=pltpu.VMEM),
        ],
        out_specs=pl.BlockSpec(memory_space=pltpu.VMEM),
        scratch_shapes=[
            pltpu.VMEM((kinds * rows * CHUNKS, LANE), jnp.float32),
            pltpu.VMEM((targets * CHUNKS, LANE), jnp.float32),
        ],
    )(idx, buf_t, fs_t, chain_part)
    return out


def gather_columns(column_block, axes):
    group = lax.axis_size(axes)
    width = column_block.shape[1]
    spread = jnp.broadcast_to(column_block[:, None, :], (column_block.shape[0], group, width))
    spread = spread.reshape(column_block.shape[0], group * width)
    return lax.all_to_all(spread, axes, split_axis=1, concat_axis=1, tiled=True)


def on_device(
    multipoles,
    up_shift,
    down_shift,
    far_shift,
    send_list,
    leaf_src,
    leaf_kind,
    coarse_src,
    coarse_kind,
):
    coefs = multipoles.shape[0]
    flat_index = lax.axis_index(("gx", "gy", "gz"))
    coarse_box = flat_index // 8
    octant = flat_index % 8
    peer_count = lax.axis_size(("gy", "gz"))
    slot_count = send_list.shape[3]
    send_order = send_list.reshape(peer_count * slot_count)
    outgoing = jnp.take(multipoles, send_order, axis=1)
    arrived = lax.all_to_all(outgoing, ("gy", "gz"), split_axis=1, concat_axis=1, tiled=True)
    upward = multipoles
    for level in range(LOCAL_LEVELS):
        upward = lift_level(upward, up_shift).astype(jnp.bfloat16)
    row_boxes = gather_columns(upward, "gz")
    row_multi = lift_level(row_boxes, up_shift).astype(jnp.bfloat16)
    coarse_multi = gather_columns(row_multi, ("gx", "gy"))
    coarse_cols = coarse_src[:, coarse_box]
    coarse_kinds = coarse_kind[:, coarse_box]
    list_len = coarse_cols.shape[0]
    coarse_picked = jnp.take(coarse_multi, coarse_cols, axis=1)
    stacked = (
        jnp.take(far_shift, coarse_kinds, axis=0)
        .transpose(1, 0, 2)
        .reshape(coefs, list_len * coefs)
    )
    column_vec = coarse_picked.transpose(1, 0).reshape(list_len * coefs, 1)
    coarse_local = jnp.dot(stacked, column_vec, preferred_element_type=jnp.float32).astype(
        jnp.bfloat16
    )
    downward = jnp.dot(down_shift[octant], coarse_local, preferred_element_type=jnp.float32).astype(
        jnp.bfloat16
    )
    for level in range(LOCAL_LEVELS - 1):
        downward = lower_level(downward, down_shift).astype(jnp.bfloat16)
    chain_part = lower_level(downward, down_shift)
    buffer = jnp.concatenate([multipoles, arrived], axis=1)
    return far_field(buffer, far_shift, leaf_src, leaf_kind, chain_part)


def solution(mesh):
    in_specs = (
        P(None, ("gx", "gy", "gz")),
        P(),
        P(),
        P(),
        P("gx", ("gy", "gz"), None, None),
        P(None, ("gx", "gy", "gz")),
        P(None, ("gx", "gy", "gz")),
        P(),
        P(),
    )
    out_specs = P(None, ("gx", "gy", "gz"))
    return jax.shard_map(
        on_device, mesh=mesh, in_specs=in_specs, out_specs=out_specs, check_vma=False
    )
```

```python
import jax
import jax.numpy as jnp
from jax import lax
from jax.experimental import pallas as pl
from jax.experimental.pallas import tpu as pltpu
from jax.sharding import PartitionSpec as P

LOCAL_LEVELS = 3
LANE = 128
CHUNKS = 3


def lift_level(children, up_shift):
    coefs = children.shape[0]
    count = children.shape[1] // 8
    child_stack = children.reshape(coefs, count, 8).transpose(2, 0, 1)
    per_octant = lax.dot_general(
        up_shift, child_stack, (((2,), (1,)), ((0,), (0,))), preferred_element_type=jnp.float32
    )
    return per_octant.sum(axis=0)


def lower_level(parent, down_shift):
    coefs = parent.shape[0]
    count = parent.shape[1]
    spread = jnp.dot(
        down_shift.reshape(8 * coefs, coefs), parent, preferred_element_type=jnp.float32
    )
    return spread.reshape(8, coefs, count).transpose(1, 2, 0).reshape(coefs, 8 * count)


def far_kernel(idx_ref, own_ref, arr_ref, fs_ref, chain_ref, out_ref, table_ref, acc_ref):
    kinds = fs_ref.shape[0]
    own = own_ref.shape[0]
    rows = own + arr_ref.shape[0]
    for k in range(kinds):
        for src_ref, first in ((own_ref, 0), (arr_ref, own)):
            whole = jnp.dot(src_ref[...], fs_ref[k], preferred_element_type=jnp.float32)
            for j in range(CHUNKS):
                table_ref[
                    pl.ds(CHUNKS * (k * rows + first) + j, src_ref.shape[0], stride=CHUNKS), :
                ] = whole[:, j * LANE : (j + 1) * LANE]
    targets = out_ref.shape[1]
    lists = idx_ref.shape[0] // targets

    def body(t, carry):
        base = t * lists
        acc = table_ref[pl.ds(idx_ref[base], CHUNKS), :]
        for l in range(1, lists):
            acc = acc + table_ref[pl.ds(idx_ref[base + l], CHUNKS), :]
        acc_ref[pl.ds(t * CHUNKS, CHUNKS), :] = acc
        return carry

    lax.fori_loop(0, targets, body, 0, unroll=8)
    coefs = out_ref.shape[0]
    for j in range(CHUNKS):
        block = acc_ref[pl.ds(j, targets, stride=CHUNKS), :].T
        used = min(LANE, coefs - j * LANE)
        near = chain_ref[pl.ds(j * LANE, used), :]
        out_ref[pl.ds(j * LANE, used), :] = (block[:used] + near).astype(out_ref.dtype)


def far_field(own_cols, arrived_cols, far_shift, leaf_src, leaf_kind, chain_part):
    coefs = own_cols.shape[0]
    rows = own_cols.shape[1] + arrived_cols.shape[1]
    kinds = far_shift.shape[0]
    lists, targets = leaf_src.shape
    width = CHUNKS * LANE
    own_t = jnp.pad(own_cols.T, ((0, 0), (0, width - coefs)))
    arr_t = jnp.pad(arrived_cols.T, ((0, 0), (0, width - coefs)))
    fs_t = jnp.pad(far_shift.transpose(0, 2, 1), ((0, 0), (0, width - coefs), (0, width - coefs)))
    idx = (CHUNKS * (leaf_kind * rows + leaf_src)).T.reshape(lists * targets)
    out = pl.pallas_call(
        far_kernel,
        out_shape=jax.ShapeDtypeStruct((coefs, targets), jnp.bfloat16),
        in_specs=[
            pl.BlockSpec(memory_space=pltpu.SMEM),
            pl.BlockSpec(memory_space=pltpu.VMEM),
            pl.BlockSpec(memory_space=pltpu.VMEM),
            pl.BlockSpec(memory_space=pltpu.VMEM),
            pl.BlockSpec(memory_space=pltpu.VMEM),
        ],
        out_specs=pl.BlockSpec(memory_space=pltpu.VMEM),
        scratch_shapes=[
            pltpu.VMEM((kinds * rows * CHUNKS, LANE), jnp.float32),
            pltpu.VMEM((targets * CHUNKS, LANE), jnp.float32),
        ],
    )(idx, own_t, arr_t, fs_t, chain_part)
    return out


def gather_columns(column_block, axes):
    group = lax.axis_size(axes)
    width = column_block.shape[1]
    spread = jnp.broadcast_to(column_block[:, None, :], (column_block.shape[0], group, width))
    spread = spread.reshape(column_block.shape[0], group * width)
    return lax.all_to_all(spread, axes, split_axis=1, concat_axis=1, tiled=True)


def on_device(
    multipoles,
    up_shift,
    down_shift,
    far_shift,
    send_list,
    leaf_src,
    leaf_kind,
    coarse_src,
    coarse_kind,
):
    coefs = multipoles.shape[0]
    flat_index = lax.axis_index(("gx", "gy", "gz"))
    coarse_box = flat_index // 8
    octant = flat_index % 8
    peer_count = lax.axis_size(("gy", "gz"))
    slot_count = send_list.shape[3]
    send_order = send_list.reshape(peer_count * slot_count)
    outgoing = jnp.take(multipoles, send_order, axis=1)
    arrived = lax.all_to_all(outgoing, ("gy", "gz"), split_axis=1, concat_axis=1, tiled=True)
    upward = multipoles
    for level in range(LOCAL_LEVELS):
        upward = lift_level(upward, up_shift).astype(jnp.bfloat16)
    row_boxes = gather_columns(upward, "gz")
    row_multi = lift_level(row_boxes, up_shift).astype(jnp.bfloat16)
    coarse_multi = gather_columns(row_multi, ("gx", "gy"))
    coarse_cols = coarse_src[:, coarse_box]
    coarse_kinds = coarse_kind[:, coarse_box]
    list_len = coarse_cols.shape[0]
    coarse_picked = jnp.take(coarse_multi, coarse_cols, axis=1)
    stacked = (
        jnp.take(far_shift, coarse_kinds, axis=0)
        .transpose(1, 0, 2)
        .reshape(coefs, list_len * coefs)
    )
    column_vec = coarse_picked.transpose(1, 0).reshape(list_len * coefs, 1)
    coarse_local = jnp.dot(stacked, column_vec, preferred_element_type=jnp.float32).astype(
        jnp.bfloat16
    )
    downward = jnp.dot(down_shift[octant], coarse_local, preferred_element_type=jnp.float32).astype(
        jnp.bfloat16
    )
    for level in range(LOCAL_LEVELS - 1):
        downward = lower_level(downward, down_shift).astype(jnp.bfloat16)
    chain_part = lower_level(downward, down_shift)
    return far_field(multipoles, arrived, far_shift, leaf_src, leaf_kind, chain_part)


def solution(mesh):
    in_specs = (
        P(None, ("gx", "gy", "gz")),
        P(),
        P(),
        P(),
        P("gx", ("gy", "gz"), None, None),
        P(None, ("gx", "gy", "gz")),
        P(None, ("gx", "gy", "gz")),
        P(),
        P(),
    )
    out_specs = P(None, ("gx", "gy", "gz"))
    return jax.shard_map(
        on_device, mesh=mesh, in_specs=in_specs, out_specs=out_specs, check_vma=False
    )
```

```python
import jax
import jax.numpy as jnp
from jax import lax
from jax.experimental import pallas as pl
from jax.experimental.pallas import tpu as pltpu
from jax.sharding import PartitionSpec as P

LOCAL_LEVELS = 3
LANE = 128
CHUNKS = 3


def lift_level(children, up_shift):
    coefs = children.shape[0]
    count = children.shape[1] // 8
    child_stack = children.reshape(coefs, count, 8).transpose(2, 0, 1)
    per_octant = lax.dot_general(
        up_shift, child_stack, (((2,), (1,)), ((0,), (0,))), preferred_element_type=jnp.float32
    )
    return per_octant.sum(axis=0)


def lower_level(parent, down_shift):
    coefs = parent.shape[0]
    count = parent.shape[1]
    spread = jnp.dot(
        down_shift.reshape(8 * coefs, coefs), parent, preferred_element_type=jnp.float32
    )
    return spread.reshape(8, coefs, count).transpose(1, 2, 0).reshape(coefs, 8 * count)


def far_kernel(idx_ref, own_ref, arr_ref, fs_ref, chain_ref, out_ref, table_ref, acc_ref):
    kinds = fs_ref.shape[0]
    own = own_ref.shape[0]
    rows = own + arr_ref.shape[0]
    for k in range(kinds):
        for src_ref, first in ((own_ref, 0), (arr_ref, own)):
            whole = jnp.dot(src_ref[...], fs_ref[k], preferred_element_type=jnp.float32)
            for j in range(CHUNKS):
                table_ref[
                    pl.ds(CHUNKS * (k * rows + first) + j, src_ref.shape[0], stride=CHUNKS), :
                ] = whole[:, j * LANE : (j + 1) * LANE]
    targets = out_ref.shape[1]
    lists = idx_ref.shape[0] // targets

    def body(t, carry):
        base = t * lists
        acc = table_ref[pl.ds(idx_ref[base], CHUNKS), :]
        for l in range(1, lists):
            acc = acc + table_ref[pl.ds(idx_ref[base + l], CHUNKS), :]
        acc_ref[pl.ds(t * CHUNKS, CHUNKS), :] = acc
        return carry

    lax.fori_loop(0, targets, body, 0, unroll=16)
    coefs = out_ref.shape[0]
    for j in range(CHUNKS):
        block = acc_ref[pl.ds(j, targets, stride=CHUNKS), :].T
        used = min(LANE, coefs - j * LANE)
        near = chain_ref[pl.ds(j * LANE, used), :]
        out_ref[pl.ds(j * LANE, used), :] = (block[:used] + near).astype(out_ref.dtype)


def far_field(own_cols, arrived_cols, far_shift, leaf_src, leaf_kind, chain_part):
    coefs = own_cols.shape[0]
    rows = own_cols.shape[1] + arrived_cols.shape[1]
    kinds = far_shift.shape[0]
    lists, targets = leaf_src.shape
    width = CHUNKS * LANE
    own_t = jnp.pad(own_cols.T, ((0, 0), (0, width - coefs)))
    arr_t = jnp.pad(arrived_cols.T, ((0, 0), (0, width - coefs)))
    fs_t = jnp.pad(far_shift.transpose(0, 2, 1), ((0, 0), (0, width - coefs), (0, width - coefs)))
    idx = (CHUNKS * (leaf_kind * rows + leaf_src)).T.reshape(lists * targets)
    out = pl.pallas_call(
        far_kernel,
        out_shape=jax.ShapeDtypeStruct((coefs, targets), jnp.bfloat16),
        in_specs=[
            pl.BlockSpec(memory_space=pltpu.SMEM),
            pl.BlockSpec(memory_space=pltpu.VMEM),
            pl.BlockSpec(memory_space=pltpu.VMEM),
            pl.BlockSpec(memory_space=pltpu.VMEM),
            pl.BlockSpec(memory_space=pltpu.VMEM),
        ],
        out_specs=pl.BlockSpec(memory_space=pltpu.VMEM),
        scratch_shapes=[
            pltpu.VMEM((kinds * rows * CHUNKS, LANE), jnp.float32),
            pltpu.VMEM((targets * CHUNKS, LANE), jnp.float32),
        ],
    )(idx, own_t, arr_t, fs_t, chain_part)
    return out


def gather_columns(column_block, axes):
    group = lax.axis_size(axes)
    width = column_block.shape[1]
    spread = jnp.broadcast_to(column_block[:, None, :], (column_block.shape[0], group, width))
    spread = spread.reshape(column_block.shape[0], group * width)
    return lax.all_to_all(spread, axes, split_axis=1, concat_axis=1, tiled=True)


def on_device(
    multipoles,
    up_shift,
    down_shift,
    far_shift,
    send_list,
    leaf_src,
    leaf_kind,
    coarse_src,
    coarse_kind,
):
    coefs = multipoles.shape[0]
    flat_index = lax.axis_index(("gx", "gy", "gz"))
    coarse_box = flat_index // 8
    octant = flat_index % 8
    peer_count = lax.axis_size(("gy", "gz"))
    slot_count = send_list.shape[3]
    send_order = send_list.reshape(peer_count * slot_count)
    outgoing = jnp.take(multipoles, send_order, axis=1)
    arrived = lax.all_to_all(outgoing, ("gy", "gz"), split_axis=1, concat_axis=1, tiled=True)
    upward = multipoles
    for level in range(LOCAL_LEVELS):
        upward = lift_level(upward, up_shift).astype(jnp.bfloat16)
    row_boxes = gather_columns(upward, "gz")
    row_multi = lift_level(row_boxes, up_shift).astype(jnp.bfloat16)
    coarse_multi = gather_columns(row_multi, ("gx", "gy"))
    coarse_cols = coarse_src[:, coarse_box]
    coarse_kinds = coarse_kind[:, coarse_box]
    list_len = coarse_cols.shape[0]
    coarse_picked = jnp.take(coarse_multi, coarse_cols, axis=1)
    stacked = (
        jnp.take(far_shift, coarse_kinds, axis=0)
        .transpose(1, 0, 2)
        .reshape(coefs, list_len * coefs)
    )
    column_vec = coarse_picked.transpose(1, 0).reshape(list_len * coefs, 1)
    coarse_local = jnp.dot(stacked, column_vec, preferred_element_type=jnp.float32).astype(
        jnp.bfloat16
    )
    downward = jnp.dot(down_shift[octant], coarse_local, preferred_element_type=jnp.float32).astype(
        jnp.bfloat16
    )
    for level in range(LOCAL_LEVELS - 1):
        downward = lower_level(downward, down_shift).astype(jnp.bfloat16)
    chain_part = lower_level(downward, down_shift)
    return far_field(multipoles, arrived, far_shift, leaf_src, leaf_kind, chain_part)


def solution(mesh):
    in_specs = (
        P(None, ("gx", "gy", "gz")),
        P(),
        P(),
        P(),
        P("gx", ("gy", "gz"), None, None),
        P(None, ("gx", "gy", "gz")),
        P(None, ("gx", "gy", "gz")),
        P(),
        P(),
    )
    out_specs = P(None, ("gx", "gy", "gz"))
    return jax.shard_map(
        on_device, mesh=mesh, in_specs=in_specs, out_specs=out_specs, check_vma=False
    )
```

```python
import jax
import jax.numpy as jnp
from jax import lax
from jax.experimental import pallas as pl
from jax.experimental.pallas import tpu as pltpu
from jax.sharding import PartitionSpec as P

LOCAL_LEVELS = 3
LANE = 128
CHUNKS = 3


def lift_level(children, up_shift):
    coefs = children.shape[0]
    count = children.shape[1] // 8
    child_stack = children.reshape(coefs, count, 8).transpose(2, 0, 1)
    per_octant = lax.dot_general(
        up_shift, child_stack, (((2,), (1,)), ((0,), (0,))), preferred_element_type=jnp.float32
    )
    return per_octant.sum(axis=0)


def lower_level(parent, down_shift):
    coefs = parent.shape[0]
    count = parent.shape[1]
    spread = jnp.dot(
        down_shift.reshape(8 * coefs, coefs), parent, preferred_element_type=jnp.float32
    )
    return spread.reshape(8, coefs, count).transpose(1, 2, 0).reshape(coefs, 8 * count)


def far_kernel(idx_ref, own_ref, arr_ref, fs_ref, chain_ref, out_ref, table_ref, acc_ref):
    kinds = fs_ref.shape[0]
    own = own_ref.shape[0]
    rows = own + arr_ref.shape[0]
    for k in range(kinds):
        for src_ref, first in ((own_ref, 0), (arr_ref, own)):
            whole = jnp.dot(src_ref[...], fs_ref[k], preferred_element_type=jnp.float32)
            for j in range(CHUNKS):
                table_ref[
                    pl.ds(CHUNKS * (k * rows + first) + j, src_ref.shape[0], stride=CHUNKS), :
                ] = whole[:, j * LANE : (j + 1) * LANE]
    targets = out_ref.shape[1]
    lists = idx_ref.shape[0] // targets

    def body(t, carry):
        base = t * lists
        acc = table_ref[pl.ds(idx_ref[base], CHUNKS), :]
        for l in range(1, lists):
            acc = acc + table_ref[pl.ds(idx_ref[base + l], CHUNKS), :]
        acc_ref[pl.ds(t * CHUNKS, CHUNKS), :] = acc
        return carry

    lax.fori_loop(0, targets, body, 0, unroll=32)
    coefs = out_ref.shape[0]
    for j in range(CHUNKS):
        block = acc_ref[pl.ds(j, targets, stride=CHUNKS), :].T
        used = min(LANE, coefs - j * LANE)
        near = chain_ref[pl.ds(j * LANE, used), :]
        out_ref[pl.ds(j * LANE, used), :] = (block[:used] + near).astype(out_ref.dtype)


def far_field(own_cols, arrived_cols, far_shift, leaf_src, leaf_kind, chain_part):
    coefs = own_cols.shape[0]
    rows = own_cols.shape[1] + arrived_cols.shape[1]
    kinds = far_shift.shape[0]
    lists, targets = leaf_src.shape
    width = CHUNKS * LANE
    own_t = jnp.pad(own_cols.T, ((0, 0), (0, width - coefs)))
    arr_t = jnp.pad(arrived_cols.T, ((0, 0), (0, width - coefs)))
    fs_t = jnp.pad(far_shift.transpose(0, 2, 1), ((0, 0), (0, width - coefs), (0, width - coefs)))
    idx = (CHUNKS * (leaf_kind * rows + leaf_src)).T.reshape(lists * targets)
    out = pl.pallas_call(
        far_kernel,
        out_shape=jax.ShapeDtypeStruct((coefs, targets), jnp.bfloat16),
        in_specs=[
            pl.BlockSpec(memory_space=pltpu.SMEM),
            pl.BlockSpec(memory_space=pltpu.VMEM),
            pl.BlockSpec(memory_space=pltpu.VMEM),
            pl.BlockSpec(memory_space=pltpu.VMEM),
            pl.BlockSpec(memory_space=pltpu.VMEM),
        ],
        out_specs=pl.BlockSpec(memory_space=pltpu.VMEM),
        scratch_shapes=[
            pltpu.VMEM((kinds * rows * CHUNKS, LANE), jnp.float32),
            pltpu.VMEM((targets * CHUNKS, LANE), jnp.float32),
        ],
    )(idx, own_t, arr_t, fs_t, chain_part)
    return out


def gather_columns(column_block, axes):
    group = lax.axis_size(axes)
    width = column_block.shape[1]
    spread = jnp.broadcast_to(column_block[:, None, :], (column_block.shape[0], group, width))
    spread = spread.reshape(column_block.shape[0], group * width)
    return lax.all_to_all(spread, axes, split_axis=1, concat_axis=1, tiled=True)


def on_device(
    multipoles,
    up_shift,
    down_shift,
    far_shift,
    send_list,
    leaf_src,
    leaf_kind,
    coarse_src,
    coarse_kind,
):
    coefs = multipoles.shape[0]
    flat_index = lax.axis_index(("gx", "gy", "gz"))
    coarse_box = flat_index // 8
    octant = flat_index % 8
    peer_count = lax.axis_size(("gy", "gz"))
    slot_count = send_list.shape[3]
    send_order = send_list.reshape(peer_count * slot_count)
    outgoing = jnp.take(multipoles, send_order, axis=1)
    arrived = lax.all_to_all(outgoing, ("gy", "gz"), split_axis=1, concat_axis=1, tiled=True)
    upward = multipoles
    for level in range(LOCAL_LEVELS):
        upward = lift_level(upward, up_shift).astype(jnp.bfloat16)
    row_boxes = gather_columns(upward, "gz")
    row_multi = lift_level(row_boxes, up_shift).astype(jnp.bfloat16)
    coarse_multi = gather_columns(row_multi, ("gx", "gy"))
    coarse_cols = coarse_src[:, coarse_box]
    coarse_kinds = coarse_kind[:, coarse_box]
    list_len = coarse_cols.shape[0]
    coarse_picked = jnp.take(coarse_multi, coarse_cols, axis=1)
    stacked = (
        jnp.take(far_shift, coarse_kinds, axis=0)
        .transpose(1, 0, 2)
        .reshape(coefs, list_len * coefs)
    )
    column_vec = coarse_picked.transpose(1, 0).reshape(list_len * coefs, 1)
    coarse_local = jnp.dot(stacked, column_vec, preferred_element_type=jnp.float32).astype(
        jnp.bfloat16
    )
    downward = jnp.dot(down_shift[octant], coarse_local, preferred_element_type=jnp.float32).astype(
        jnp.bfloat16
    )
    for level in range(LOCAL_LEVELS - 1):
        downward = lower_level(downward, down_shift).astype(jnp.bfloat16)
    chain_part = lower_level(downward, down_shift)
    return far_field(multipoles, arrived, far_shift, leaf_src, leaf_kind, chain_part)


def solution(mesh):
    in_specs = (
        P(None, ("gx", "gy", "gz")),
        P(),
        P(),
        P(),
        P("gx", ("gy", "gz"), None, None),
        P(None, ("gx", "gy", "gz")),
        P(None, ("gx", "gy", "gz")),
        P(),
        P(),
    )
    out_specs = P(None, ("gx", "gy", "gz"))
    return jax.shard_map(
        on_device, mesh=mesh, in_specs=in_specs, out_specs=out_specs, check_vma=False
    )
```

```python
import jax
import jax.numpy as jnp
from jax import lax
from jax.experimental import pallas as pl
from jax.experimental.pallas import tpu as pltpu
from jax.sharding import PartitionSpec as P

LOCAL_LEVELS = 3
LANE = 128
CHUNKS = 3


def lift_level(children, up_shift):
    coefs = children.shape[0]
    count = children.shape[1] // 8
    child_stack = children.reshape(coefs, count, 8).transpose(2, 0, 1)
    per_octant = lax.dot_general(
        up_shift, child_stack, (((2,), (1,)), ((0,), (0,))), preferred_element_type=jnp.float32
    )
    return per_octant.sum(axis=0)


def lower_level(parent, down_shift):
    coefs = parent.shape[0]
    count = parent.shape[1]
    spread = jnp.dot(
        down_shift.reshape(8 * coefs, coefs), parent, preferred_element_type=jnp.float32
    )
    return spread.reshape(8, coefs, count).transpose(1, 2, 0).reshape(coefs, 8 * count)


def far_kernel(idx_ref, own_ref, arr_ref, fs_ref, chain_ref, out_ref, table_ref, acc_ref):
    kinds = fs_ref.shape[0]
    own = own_ref.shape[0]
    rows = own + arr_ref.shape[0]
    for k in range(kinds):
        for src_ref, first in ((own_ref, 0), (arr_ref, own)):
            whole = jnp.dot(src_ref[...], fs_ref[k], preferred_element_type=jnp.float32)
            for j in range(CHUNKS):
                table_ref[
                    pl.ds(CHUNKS * (k * rows + first) + j, src_ref.shape[0], stride=CHUNKS), :
                ] = whole[:, j * LANE : (j + 1) * LANE]
    targets = out_ref.shape[1]
    lists = idx_ref.shape[0] // targets

    def body(t, carry):
        base = t * lists
        half = lists // 2
        acc = table_ref[pl.ds(idx_ref[base], CHUNKS), :]
        other = table_ref[pl.ds(idx_ref[base + half], CHUNKS), :]
        for l in range(1, half):
            acc = acc + table_ref[pl.ds(idx_ref[base + l], CHUNKS), :]
            other = other + table_ref[pl.ds(idx_ref[base + half + l], CHUNKS), :]
        acc = acc + other
        acc_ref[pl.ds(t * CHUNKS, CHUNKS), :] = acc
        return carry

    lax.fori_loop(0, targets, body, 0, unroll=16)
    coefs = out_ref.shape[0]
    for j in range(CHUNKS):
        block = acc_ref[pl.ds(j, targets, stride=CHUNKS), :].T
        used = min(LANE, coefs - j * LANE)
        near = chain_ref[pl.ds(j * LANE, used), :]
        out_ref[pl.ds(j * LANE, used), :] = (block[:used] + near).astype(out_ref.dtype)


def far_field(own_cols, arrived_cols, far_shift, leaf_src, leaf_kind, chain_part):
    coefs = own_cols.shape[0]
    rows = own_cols.shape[1] + arrived_cols.shape[1]
    kinds = far_shift.shape[0]
    lists, targets = leaf_src.shape
    width = CHUNKS * LANE
    own_t = jnp.pad(own_cols.T, ((0, 0), (0, width - coefs)))
    arr_t = jnp.pad(arrived_cols.T, ((0, 0), (0, width - coefs)))
    fs_t = jnp.pad(far_shift.transpose(0, 2, 1), ((0, 0), (0, width - coefs), (0, width - coefs)))
    idx = (CHUNKS * (leaf_kind * rows + leaf_src)).T.reshape(lists * targets)
    out = pl.pallas_call(
        far_kernel,
        out_shape=jax.ShapeDtypeStruct((coefs, targets), jnp.bfloat16),
        in_specs=[
            pl.BlockSpec(memory_space=pltpu.SMEM),
            pl.BlockSpec(memory_space=pltpu.VMEM),
            pl.BlockSpec(memory_space=pltpu.VMEM),
            pl.BlockSpec(memory_space=pltpu.VMEM),
            pl.BlockSpec(memory_space=pltpu.VMEM),
        ],
        out_specs=pl.BlockSpec(memory_space=pltpu.VMEM),
        scratch_shapes=[
            pltpu.VMEM((kinds * rows * CHUNKS, LANE), jnp.float32),
            pltpu.VMEM((targets * CHUNKS, LANE), jnp.float32),
        ],
    )(idx, own_t, arr_t, fs_t, chain_part)
    return out


def gather_columns(column_block, axes):
    group = lax.axis_size(axes)
    width = column_block.shape[1]
    spread = jnp.broadcast_to(column_block[:, None, :], (column_block.shape[0], group, width))
    spread = spread.reshape(column_block.shape[0], group * width)
    return lax.all_to_all(spread, axes, split_axis=1, concat_axis=1, tiled=True)


def on_device(
    multipoles,
    up_shift,
    down_shift,
    far_shift,
    send_list,
    leaf_src,
    leaf_kind,
    coarse_src,
    coarse_kind,
):
    coefs = multipoles.shape[0]
    flat_index = lax.axis_index(("gx", "gy", "gz"))
    coarse_box = flat_index // 8
    octant = flat_index % 8
    peer_count = lax.axis_size(("gy", "gz"))
    slot_count = send_list.shape[3]
    send_order = send_list.reshape(peer_count * slot_count)
    outgoing = jnp.take(multipoles, send_order, axis=1)
    arrived = lax.all_to_all(outgoing, ("gy", "gz"), split_axis=1, concat_axis=1, tiled=True)
    upward = multipoles
    for level in range(LOCAL_LEVELS):
        upward = lift_level(upward, up_shift).astype(jnp.bfloat16)
    row_boxes = gather_columns(upward, "gz")
    row_multi = lift_level(row_boxes, up_shift).astype(jnp.bfloat16)
    coarse_multi = gather_columns(row_multi, ("gx", "gy"))
    coarse_cols = coarse_src[:, coarse_box]
    coarse_kinds = coarse_kind[:, coarse_box]
    list_len = coarse_cols.shape[0]
    coarse_picked = jnp.take(coarse_multi, coarse_cols, axis=1)
    stacked = (
        jnp.take(far_shift, coarse_kinds, axis=0)
        .transpose(1, 0, 2)
        .reshape(coefs, list_len * coefs)
    )
    column_vec = coarse_picked.transpose(1, 0).reshape(list_len * coefs, 1)
    coarse_local = jnp.dot(stacked, column_vec, preferred_element_type=jnp.float32).astype(
        jnp.bfloat16
    )
    downward = jnp.dot(down_shift[octant], coarse_local, preferred_element_type=jnp.float32).astype(
        jnp.bfloat16
    )
    for level in range(LOCAL_LEVELS - 1):
        downward = lower_level(downward, down_shift).astype(jnp.bfloat16)
    chain_part = lower_level(downward, down_shift)
    return far_field(multipoles, arrived, far_shift, leaf_src, leaf_kind, chain_part)


def solution(mesh):
    in_specs = (
        P(None, ("gx", "gy", "gz")),
        P(),
        P(),
        P(),
        P("gx", ("gy", "gz"), None, None),
        P(None, ("gx", "gy", "gz")),
        P(None, ("gx", "gy", "gz")),
        P(),
        P(),
    )
    out_specs = P(None, ("gx", "gy", "gz"))
    return jax.shard_map(
        on_device, mesh=mesh, in_specs=in_specs, out_specs=out_specs, check_vma=False
    )
```
